512 devices in a mesh: owner: 16 (over x, y_hi), beam: 32 (over y_lo, z, core).
Axes of the slice: x: 4, y: 8 (y_hi: 4, y_lo: 2; y = y_hi * 2 + y_lo), z: 8, core: 2. Of those that a mesh axis runs over, the one named last changes fastest.
Arguments:
- hidden: bfloat16 [4096, 8192], P('owner'), may hold values from -6 to 6
- norm_gain: bfloat16 [8192], replicated, may hold values from 0.099609375 to 1.8984375
- w_qkv: bfloat16 [8192, 10240], P('owner', 'beam'), may hold values from -0.0625 to 0.0625
- w_out: bfloat16 [8192, 8192], P('beam', 'owner'), may hold values from -0.125 to 0.125
- kv_cache: bfloat16 [16384, 2, 8, 1024], P(('owner', 'beam')), may hold values from -384 to 384
- lengths: int32 [4096], P('owner'), may hold values from 1 to 32, 98304 in all
- kept_parent_device: int32 [16384, 1], P('owner'), may hold values from 0 to 31; in each aligned block of 32 rows (0 to 31, 32 to 63, ...) at most 2 rows name the same one
- keep_block: int32 [16384], P('owner'), may hold values from 0 to 31
Outputs:
- mixed: bfloat16 [4096, 8192], P('owner', 'beam')
The draws below stay inside these ranges and needn't reach their ends.
Inputs may be any that keep to these rules, and one draw needn't show every extreme that they name: `kept_parent_device`: in each aligned block of 32 entries (the new blocks of one device) no value appears more than 2 times, and some value appears exactly 2 times in some block. `lengths`: each entry is at least 1; the largest is exactly 32.
All inputs are finite; a program needn't handle non-finite values. No bound on the sum of `lengths` on one device may be relied on, other than what follows from the above.
Results may differ from the reference program's by a relative error of at most 0.024.
Values may be sent and summed in bfloat16 or wider, within the bound.
No kernel may reach another device: no remote copies, remote signals or barrier semaphores. Data moves between devices by JAX's collectives and lax.ppermute only.
A program may use at most 64 MiB of HBM per device.

```python
import math
import jax
import jax.numpy as jnp
import numpy as np
from jax import lax

D = 8192
QH = 64
KVH = 8
HD = 128
CACHE = 32
PAGE = 8
QKV = 10240
NB = 4
BLK_DEV = 32
BEAMS = 4096
BLOCKS = 16384
HSHARD = 256
MOST = 2
N_BEAM = 32


def draw_kv_cache(key, part):
    first_key = jax.random.fold_in(jax.random.fold_in(key, 7), 0)
    shape = (BLOCKS, 2, PAGE, KVH * HD)
    base = jnp.clip(jax.random.normal(first_key, shape, jnp.float32), -6.0, 6.0)
    return base.astype(jnp.bfloat16)


def set_ends(entries, key, smallest, high):
    longest = entries.shape.index(max(entries.shape))
    spots = []
    for shift in (0, 1):
        where = [jax.random.randint(jax.random.fold_in(key, axis), (), 0, length) for axis, length in enumerate(entries.shape)]
        where[longest] = (where[longest] + shift) % entries.shape[longest]
        spots.append(tuple(where))
    return entries.at[spots[0]].set(smallest).at[spots[1]].set(high)


def strengthened(values, own_key, source, target, shards_of, factor):
    owner, partner = [(jnp.arange(values.shape[position]) // (values.shape[position] // shards_of)).reshape([-1 if axis == position else 1 for axis in range(values.ndim)]) for position in (source, target)]
    chosen = jax.random.permutation(own_key, shards_of)[partner]
    strong = (owner == chosen) | (owner == (partner + shards_of // 2) % shards_of)
    return jnp.where(strong, factor * values, values)


def block_scale(rng, extent, pieces, low, top_value):
    level, own = 1.0, jax.random.fold_in(rng, 6)
    for dim, parts in pieces:
        heights = jnp.exp(jax.random.uniform(jax.random.fold_in(own, dim), (parts,), jnp.float32, low / len(pieces), top_value / len(pieces)))
        level = level * jnp.repeat(heights, extent[dim] // parts).reshape([-1 if axis == dim else 1 for axis in range(len(extent))])
    return level


def profile(count, total, reach, slope):
    weights = [(1 << 20) // math.isqrt(standing ** slope) + 1 for standing in range(2, count + 1)]
    rest, holding = total - reach - (count - 1), [1] * (count - 1)
    while rest > 0:
        movable = [i for i in range(count - 1) if holding[i] < reach]
        whole, remaining = sum([weights[i] for i in movable]), rest
        for i in movable:
            extra = min(reach - holding[i], max(1, remaining * weights[i] // whole), rest)
            holding[i] = holding[i] + extra
            rest = rest - extra
    return np.array([reach] + holding)


def uneven_parts(rng, count, total, limit, skew):
    if count == 2:
        one = jax.random.randint(rng, (), max(1, total - limit), min(limit, total - 1) + 1)
        return jnp.stack([one, total - one])
    sizes = jnp.asarray(profile(count, total, limit, skew), jnp.int32)
    twos = (count - 1) // 2
    donor, sink = sizes[1:1 + 2 * twos:2], sizes[2:2 + 2 * twos:2]
    slack = jnp.minimum(donor - 1, limit - sink)
    moved = jax.random.randint(jax.random.fold_in(rng, 1), (twos,), 0, 1 << 20) % (slack + 1)
    sizes = sizes.at[1:1 + 2 * twos:2].set(donor - moved).at[2:2 + 2 * twos:2].set(sink + moved)
    return sizes[jax.random.permutation(jax.random.fold_in(rng, 2), count)]


def shared_out(rng, own, number, rows, amount, top, reach, skew):
    ranking = jax.random.permutation(rng, amount)
    packed, usual = load_shares(amount, rows * top, reach, skew, True), load_shares(amount, rows * top, reach, skew, False)
    places = jnp.arange(amount)

    def named(sizes, turn):
        used = int((sizes > 0).sum())
        fixed = max(1, used // 4)
        passed = fixed + (places - fixed + turn * (used - fixed)) % max(1, amount - fixed)
        return jnp.zeros((amount,), jnp.int32).at[ranking[jnp.where(places < fixed, places, passed)]].set(jnp.asarray(sizes, jnp.int32))

    sizes = jnp.where(number % 4 == 0, named(packed, number // 4), named(usual, number - number // 4 - 1))
    mixed = jax.random.permutation(jax.random.fold_in(own, 3), amount)
    donor, taker = mixed[0:amount // 2 * 2:2], mixed[1:amount // 2 * 2:2]
    slack = jnp.minimum(sizes[donor] - 1, reach - sizes[taker]) // 2
    slack = jnp.where((donor == ranking[0]) | (taker == ranking[0]) | (sizes[taker] == 0), 0, jnp.maximum(slack, 0))
    passed = jax.random.randint(jax.random.fold_in(own, 4), (amount // 2,), 0, 1 << 20) % (slack + 1)
    sizes = sizes.at[donor].add(-passed).at[taker].add(passed)
    items = jnp.searchsorted(jnp.cumsum(sizes), jnp.arange(rows * top), side="right").astype(jnp.int32)
    listing = items.reshape(top, rows).T
    listing = listing[jax.random.permutation(jax.random.fold_in(own, 1), rows)]
    turn = jax.random.randint(jax.random.fold_in(own, 2), (rows, 1), 0, top)
    return jnp.take_along_axis(listing, (jnp.arange(top)[None, :] + turn) % top, axis=1)


def load_shares(number_of, total, bound, lean, full):
    loads = [(1 << 20) // math.isqrt(grade ** lean) + 1 for grade in range(1, number_of + 1)]
    largest = bound if full else min(bound, max(-(-total // number_of), total * loads[0] // sum(loads)))
    least = 1 if total - largest >= number_of - 1 else 0
    given, surplus = [largest] + [least] * (number_of - 1), total - largest - least * (number_of - 1)
    while surplus > 0:
        candidates = [i for i in range(1, number_of) if given[i] < largest] or [i for i in range(1, number_of) if given[i] < bound]
        pool, budget = sum([loads[i] for i in candidates]), surplus
        for i in candidates:
            more = min(bound - given[i], max(1, budget * loads[i] // pool), surplus)
            given[i] = given[i] + more
            surplus = surplus - more
    return np.array(given)


def centred(own_key, extent, width, reach, shards=(), kind=jnp.bfloat16):
    array = width * jax.random.normal(own_key, extent, jnp.float32)
    if shards:
        array = array * block_scale(own_key, extent, shards, -0.22, 0.18)
    return jnp.clip(array, -reach, reach).astype(kind)


def heavy_noise(stream_key, dims, scale, most, cuts, heavy, held_as=jnp.bfloat16):
    values = scale * jax.random.normal(stream_key, dims, jnp.float32)
    if cuts:
        values = values * block_scale(stream_key, dims, cuts, -0.22, 0.18)
    return jnp.clip(strengthened(values, jax.random.fold_in(stream_key, 3), *heavy), -most, most).astype(held_as)


def setup_inputs(seed: int = 0) -> dict:
    streams_of = jax.random.split(jax.random.key(seed), 9)
    hidden = centred(streams_of[0], (BEAMS, D), 1.0, 6.0, ((0, 16),))
    norm_gain = jnp.clip(1.0 + 0.18 * jax.random.normal(streams_of[1], (D,), jnp.float32), 0.099609375, 1.8984375).astype(jnp.bfloat16)
    w_qkv = centred(streams_of[2], (D, QKV), D ** -0.5, 0.0625, ((0, 16), (1, 32)))
    w_out = heavy_noise(streams_of[3], (QH * HD, D), (QH * HD) ** -0.5, 0.125, ((0, 32), (1, 16)), (0, 1, 32, 2.75))
    kv_cache = draw_kv_cache(jax.random.fold_in(streams_of[8], 71), 0)
    lengths = uneven_parts(streams_of[5], BEAMS, BEAMS * CACHE * 3 // 4, CACHE, 2).astype(jnp.int32)
    kept_parent_device_keys = jax.random.split(jax.random.fold_in(streams_of[6], 1), BLOCKS // BLK_DEV)
    kept_parent_device_turns = jax.random.permutation(jax.random.fold_in(streams_of[6], 3), BLOCKS // BLK_DEV)
    kept_parent_device = jax.vmap(lambda own, number: shared_out(jax.random.fold_in(streams_of[6], 2), own, number, BLK_DEV, N_BEAM, 1, MOST, 2))(kept_parent_device_keys, kept_parent_device_turns).reshape((BLOCKS, 1))
    keep_block = set_ends(jax.random.randint(streams_of[7], (BLOCKS,), 0, BLK_DEV), jax.random.fold_in(streams_of[7], 1), 0, BLK_DEV - 1).astype(jnp.int32)
    return {"hidden": hidden, "norm_gain": norm_gain, "w_qkv": w_qkv, "w_out": w_out, "kv_cache": kv_cache, "lengths": lengths, "kept_parent_device": kept_parent_device, "keep_block": keep_block}


def rotary_embed(values, positions):
    half = values.shape[-1] // 2
    freqs = 500000.0 ** (-(jnp.arange(half, dtype=jnp.float32) * 2.0) / values.shape[-1])
    angles = positions.astype(jnp.float32)[:, None] * freqs[None, :]
    cosine = jnp.cos(angles)[:, None, :]
    sine = jnp.sin(angles)[:, None, :]
    first = values[..., :half]
    second = values[..., half:]
    return jnp.concatenate([first * cosine - second * sine, second * cosine + first * sine], axis=-1)

def attend(queries, fresh_key, value_new, keys, values, positions):
    beams = queries.shape[0]
    grouped_heads = queries.reshape(beams, KVH, QH // KVH, HD).astype(jnp.float32)
    scale_factor = HD ** (-0.5)
    scores = jnp.einsum('bkgd,btkd->bkgt', grouped_heads, keys.astype(jnp.float32)) * scale_factor
    local_beam_score = jnp.einsum('rhap,rhp->rha', grouped_heads, fresh_key.astype(jnp.float32)) * scale_factor
    valid = (jnp.arange(CACHE, dtype=jnp.int32)[None, :] < positions[:, None])[:, None, None, :]
    scores = jnp.where(valid, scores, -1e+30)
    highest = jnp.maximum(lax.optimization_barrier(jnp.max(scores, axis=-1)), local_beam_score)
    weights = jnp.where(valid, jnp.exp(scores - highest[..., None]), 0.0)
    own_weight = jnp.exp(local_beam_score - highest)
    totals = lax.optimization_barrier(jnp.sum(weights, axis=-1)) + own_weight
    probs = (weights / totals[..., None]).astype(jnp.bfloat16)
    own_prob = (own_weight / totals).astype(jnp.bfloat16)
    output = jnp.einsum('bkgt,btkd->bkgd', probs.astype(jnp.float32), values.astype(jnp.float32))
    output = output + own_prob.astype(jnp.float32)[..., None] * value_new.astype(jnp.float32)[:, :, None, :]
    return output.reshape(beams, QH * HD).astype(jnp.bfloat16)

def reference(hidden, norm_gain, w_qkv, w_out, kv_cache, lengths, kept_parent_device, keep_block):
    floats = hidden.astype(jnp.float32)
    scale_rms = lax.rsqrt(lax.optimization_barrier(jnp.mean(floats * floats, axis=-1, keepdims=True)) + 1e-05)
    normed = (floats * scale_rms * norm_gain.astype(jnp.float32)).astype(jnp.bfloat16)
    qkv = jnp.dot(normed, w_qkv, preferred_element_type=jnp.float32).astype(jnp.bfloat16)
    query_cols = qkv[:, :QH * HD].reshape(BEAMS, QH, HD).astype(jnp.float32)
    key_cols = qkv[:, QH * HD:(QH + KVH) * HD].reshape(BEAMS, KVH, HD).astype(jnp.float32)
    value_new = qkv[:, (QH + KVH) * HD:].reshape(BEAMS, KVH, HD)
    queries = rotary_embed(query_cols, lengths).astype(jnp.bfloat16)
    fresh_key = rotary_embed(key_cols, lengths).astype(jnp.bfloat16)
    block_ids = jnp.arange(BLOCKS, dtype=jnp.int32)
    group_base = block_ids // (N_BEAM * BLK_DEV) * (N_BEAM * BLK_DEV)
    sources = (group_base + kept_parent_device[:, 0] * BLK_DEV + keep_block).astype(jnp.int32)
    moved = kv_cache[sources].reshape(BEAMS, NB, 2, PAGE, KVH, HD)
    keys = moved[:, :, 0].reshape(BEAMS, CACHE, KVH, HD)
    values = moved[:, :, 1].reshape(BEAMS, CACHE, KVH, HD)
    attn = attend(queries, fresh_key, value_new, keys, values, lengths)
    running = jnp.zeros((BEAMS, D), jnp.float32)
    for shard in range(N_BEAM):
        partial_sum = jnp.dot(attn[:, shard * HSHARD:(shard + 1) * HSHARD], w_out[shard * HSHARD:(shard + 1) * HSHARD], preferred_element_type=jnp.float32)
        rounded = lax.optimization_barrier(partial_sum.astype(jnp.bfloat16))
        running = running + rounded.astype(jnp.float32)
    return running.astype(jnp.bfloat16)
```

```python
import jax
import jax.numpy as jnp
from jax import lax
from jax.sharding import Mesh
from jax.sharding import PartitionSpec as P

QH = 64
KVH = 8
HD = 128
CACHE = 32
PAGE = 8
QKV = 10240

OWNER = ("x", "yh")
BEAM = ("yl", "z", "c")
PAIR = ("yl", "z")


def rotary_embed(values, positions):
    half = values.shape[-1] // 2
    freqs = 500000.0 ** (-(jnp.arange(half, dtype=jnp.float32) * 2.0) / values.shape[-1])
    angles = positions.astype(jnp.float32)[:, None] * freqs[None, :]
    cosine = jnp.cos(angles)[:, None, :]
    sine = jnp.sin(angles)[:, None, :]
    first = values[..., :half]
    second = values[..., half:]
    return jnp.concatenate(
        [first * cosine - second * sine, second * cosine + first * sine], axis=-1
    )


def regroup(blocks):
    return lax.all_to_all(blocks, BEAM, split_axis=1, concat_axis=1, tiled=True)


def gather_rows(tile, axis, count):
    copies = jnp.broadcast_to(tile[None], (count,) + tile.shape)
    return lax.all_to_all(copies, axis, 0, 0, tiled=True).reshape((-1,) + tile.shape[1:])


def attend(queries, fresh_key, value_new, keys, values, positions):
    beams = queries.shape[0]
    grouped_heads = queries.reshape(beams, KVH, QH // KVH, HD)
    scale_factor = HD ** (-0.5)
    scores = (
        jnp.einsum("bkgd,btkd->bkgt", grouped_heads, keys, preferred_element_type=jnp.float32)
        * scale_factor
    )
    local_beam_score = (
        jnp.einsum("rhap,rhp->rha", grouped_heads, fresh_key, preferred_element_type=jnp.float32)
        * scale_factor
    )
    valid = (jnp.arange(keys.shape[1], dtype=jnp.int32)[None, :] < positions[:, None])[
        :, None, None, :
    ]
    scores = jnp.where(valid, scores, -1e30)
    highest = jnp.maximum(jnp.max(scores, axis=-1), local_beam_score)
    weights = jnp.where(valid, jnp.exp(scores - highest[..., None]), 0.0)
    own_weight = jnp.exp(local_beam_score - highest)
    totals = jnp.sum(weights, axis=-1) + own_weight
    probs = (weights / totals[..., None]).astype(jnp.bfloat16)
    own_prob = (own_weight / totals).astype(jnp.bfloat16)
    output = jnp.einsum("bkgt,btkd->bkgd", probs, values, preferred_element_type=jnp.float32)
    output = (
        output
        + own_prob.astype(jnp.float32)[..., None] * value_new.astype(jnp.float32)[:, :, None, :]
    )
    return output.reshape(beams, QH * HD).astype(jnp.bfloat16)


def shards(hidden, norm_gain, w_qkv, w_out, kv_cache, lengths, kept_parent_device, keep_block):
    columns = lax.axis_size(BEAM)
    my_column = lax.axis_index(BEAM)
    grouped_row_block = hidden.shape[0]
    own_beams = grouped_row_block // columns
    w_piece = lax.all_gather(w_out, OWNER, axis=1, tiled=True)
    full_w = gather_rows(gather_rows(w_qkv, "yh", lax.axis_size("yh")), "x", lax.axis_size("x"))
    floats = hidden.astype(jnp.float32)
    scale_rms = lax.rsqrt(jnp.mean(floats * floats, axis=-1, keepdims=True) + 1e-05)
    normed = (floats * scale_rms * norm_gain.astype(jnp.float32)).astype(jnp.bfloat16)
    normed_split = normed.reshape(columns, own_beams, normed.shape[1])
    projected = jnp.einsum(
        "jbd,dc->bjc", normed_split, full_w, preferred_element_type=jnp.float32
    )
    own_qkv = regroup(projected.astype(jnp.bfloat16)).reshape(own_beams, QKV)
    blk_dev = kv_cache.shape[0]
    most_slots = max(2, 2 * blk_dev // columns)
    sources = kept_parent_device.reshape(columns, blk_dev)
    picked = keep_block.reshape(columns, blk_dev)
    is_mine = (sources == my_column).astype(jnp.int32)
    ranks = jnp.cumsum(is_mine, axis=1) - 1
    slot_ids = jnp.arange(most_slots, dtype=jnp.int32)
    chosen = is_mine[:, :, None] * (ranks[:, :, None] == slot_ids[None, None, :]).astype(jnp.int32)
    send_table = jnp.sum(chosen * picked[:, :, None], axis=1)
    outgoing = kv_cache[send_table.reshape(-1)].reshape((columns, most_slots) + kv_cache.shape[1:])
    incoming_blocks = lax.all_to_all(outgoing, BEAM, split_axis=0, concat_axis=0, tiled=True)
    own_sources = lax.dynamic_index_in_dim(sources, my_column, 0, keepdims=False)
    one_hot = (own_sources[:, None] == jnp.arange(columns, dtype=jnp.int32)[None, :]).astype(
        jnp.int32
    )
    earlier = jnp.cumsum(one_hot, axis=0) - one_hot
    arrival = jnp.sum(earlier * one_hot, axis=1)
    flat_blocks = incoming_blocks.reshape((columns * most_slots,) + kv_cache.shape[1:])
    moved = flat_blocks[own_sources * most_slots + arrival]
    moved = moved.reshape(own_beams, CACHE // PAGE, 2, PAGE, KVH, HD)
    keys = moved[:, :, 0].reshape(own_beams, CACHE, KVH, HD)
    values = moved[:, :, 1].reshape(own_beams, CACHE, KVH, HD)
    positions = lax.dynamic_slice_in_dim(lengths, my_column * own_beams, own_beams)
    query_cols = own_qkv[:, : QH * HD].reshape(own_beams, QH, HD).astype(jnp.float32)
    key_cols = own_qkv[:, QH * HD : (QH + KVH) * HD].reshape(own_beams, KVH, HD).astype(jnp.float32)
    value_new = own_qkv[:, (QH + KVH) * HD :].reshape(own_beams, KVH, HD)
    queries = rotary_embed(query_cols, positions).astype(jnp.bfloat16)
    fresh_key = rotary_embed(key_cols, positions).astype(jnp.bfloat16)
    attn = attend(queries, fresh_key, value_new, keys, values, positions)
    head_rows = regroup(attn.reshape(own_beams, columns, attn.shape[1] // columns))
    terms = jnp.einsum(
        "bjh,hc->jbc", head_rows, w_piece, preferred_element_type=jnp.float32
    ).reshape(grouped_row_block, w_piece.shape[1]).astype(jnp.bfloat16)
    cores = lax.axis_size("c")
    core = lax.axis_index("c")
    width = terms.shape[1] // columns
    split = terms.reshape(grouped_row_block, columns // cores, cores, width)
    kept = jnp.take(split, core, axis=2)
    sent = jnp.take(split, 1 - core, axis=2)
    got = lax.ppermute(sent, "c", [(0, 1), (1, 0)])
    pair = (kept.astype(jnp.float32) + got.astype(jnp.float32)).astype(jnp.bfloat16)
    spread = lax.all_to_all(pair.transpose(1, 0, 2), PAIR, 0, 0, tiled=True)
    return jnp.sum(spread.astype(jnp.float32), axis=0).astype(jnp.bfloat16)


def solution(mesh):
    sizes = dict(mesh.shape)
    parts = mesh.devices.reshape(4, sizes["owner"] // 4, 2, sizes["beam"] // 4, 2)
    view = Mesh(parts, OWNER + BEAM)
    return jax.shard_map(
        shards,
        mesh=view,
        in_specs=(
            P(OWNER, None),
            P(),
            P(OWNER, BEAM),
            P(BEAM, OWNER),
            P(OWNER + BEAM, None, None, None),
            P(OWNER),
            P(OWNER, None),
            P(OWNER),
        ),
        out_specs=P(OWNER, BEAM),
        check_vma=False,
    )
```

```python
import jax
import jax.numpy as jnp
from jax import lax
from jax.sharding import Mesh
from jax.sharding import PartitionSpec as P

QH = 64
KVH = 8
HD = 128
CACHE = 32
PAGE = 8
QKV = 10240

OWNER = ("x", "yh")
BEAM = ("yl", "z", "c")
PAIR = ("yl", "z")


def rotary_embed(values, positions):
    half = values.shape[-1] // 2
    freqs = 500000.0 ** (-(jnp.arange(half, dtype=jnp.float32) * 2.0) / values.shape[-1])
    angles = positions.astype(jnp.float32)[:, None] * freqs[None, :]
    cosine = jnp.cos(angles)[:, None, :]
    sine = jnp.sin(angles)[:, None, :]
    first = values[..., :half]
    second = values[..., half:]
    return jnp.concatenate(
        [first * cosine - second * sine, second * cosine + first * sine], axis=-1
    )


def regroup(blocks):
    return lax.all_to_all(blocks, BEAM, split_axis=1, concat_axis=1, tiled=True)


def gather_rows(tile, axis, count):
    copies = jnp.broadcast_to(tile[None], (count,) + tile.shape)
    return lax.all_to_all(copies, axis, 0, 0, tiled=True).reshape((-1,) + tile.shape[1:])


def attend(queries, fresh_key, value_new, keys, values, positions):
    beams = queries.shape[0]
    grouped_heads = queries.reshape(beams, KVH, QH // KVH, HD)
    scale_factor = HD ** (-0.5)
    scores = (
        jnp.einsum("bkgd,btkd->bkgt", grouped_heads, keys, preferred_element_type=jnp.float32)
        * scale_factor
    )
    local_beam_score = (
        jnp.einsum("rhap,rhp->rha", grouped_heads, fresh_key, preferred_element_type=jnp.float32)
        * scale_factor
    )
    valid = (jnp.arange(keys.shape[1], dtype=jnp.int32)[None, :] < positions[:, None])[
        :, None, None, :
    ]
    scores = jnp.where(valid, scores, -1e30)
    highest = jnp.maximum(jnp.max(scores, axis=-1), local_beam_score)
    weights = jnp.where(valid, jnp.exp(scores - highest[..., None]), 0.0)
    own_weight = jnp.exp(local_beam_score - highest)
    totals = jnp.sum(weights, axis=-1) + own_weight
    probs = (weights / totals[..., None]).astype(jnp.bfloat16)
    own_prob = (own_weight / totals).astype(jnp.bfloat16)
    output = jnp.einsum("bkgt,btkd->bkgd", probs, values, preferred_element_type=jnp.float32)
    output = (
        output
        + own_prob.astype(jnp.float32)[..., None] * value_new.astype(jnp.float32)[:, :, None, :]
    )
    return output.reshape(beams, QH * HD).astype(jnp.bfloat16)


def shards(hidden, norm_gain, w_qkv, w_out, kv_cache, lengths, kept_parent_device, keep_block):
    columns = lax.axis_size(BEAM)
    my_column = lax.axis_index(BEAM)
    grouped_row_block = hidden.shape[0]
    own_beams = grouped_row_block // columns
    halves = w_out.reshape(w_out.shape[0], lax.axis_size("c"), w_out.shape[1] // lax.axis_size("c"))
    w_local = lax.all_to_all(halves, "c", 1, 0, tiled=True).reshape(-1, halves.shape[2])
    w_pair = lax.all_gather(w_local, OWNER, axis=1, tiled=False)
    xs = lax.axis_size("x")
    full_w = lax.all_to_all(
        jnp.broadcast_to(gather_rows(w_qkv, "yh", lax.axis_size("yh"))[None], (xs, w_qkv.shape[0] * lax.axis_size("yh"), w_qkv.shape[1])),
        "x", 0, 0, tiled=True,
    )
    floats = hidden.astype(jnp.float32)
    scale_rms = lax.rsqrt(jnp.mean(floats * floats, axis=-1, keepdims=True) + 1e-05)
    normed = (floats * scale_rms * norm_gain.astype(jnp.float32)).astype(jnp.bfloat16)
    normed_split = normed.reshape(columns, own_beams, full_w.shape[0], full_w.shape[1])
    projected = jnp.einsum(
        "jbxd,xdc->bjc", normed_split, full_w, preferred_element_type=jnp.float32
    )
    own_qkv = regroup(projected.astype(jnp.bfloat16)).reshape(own_beams, QKV)
    blk_dev = kv_cache.shape[0]
    most_slots = max(2, 2 * blk_dev // columns)
    sources = kept_parent_device.reshape(columns, blk_dev)
    picked = keep_block.reshape(columns, blk_dev)
    is_mine = (sources == my_column).astype(jnp.int32)
    ranks = jnp.cumsum(is_mine, axis=1) - 1
    slot_ids = jnp.arange(most_slots, dtype=jnp.int32)
    chosen = is_mine[:, :, None] * (ranks[:, :, None] == slot_ids[None, None, :]).astype(jnp.int32)
    send_table = jnp.sum(chosen * picked[:, :, None], axis=1)
    outgoing = kv_cache[send_table.reshape(-1)].reshape((columns, most_slots) + kv_cache.shape[1:])
    incoming_blocks = lax.all_to_all(outgoing, BEAM, split_axis=0, concat_axis=0, tiled=True)
    own_sources = lax.dynamic_index_in_dim(sources, my_column, 0, keepdims=False)
    one_hot = (own_sources[:, None] == jnp.arange(columns, dtype=jnp.int32)[None, :]).astype(
        jnp.int32
    )
    earlier = jnp.cumsum(one_hot, axis=0) - one_hot
    arrival = jnp.sum(earlier * one_hot, axis=1)
    flat_blocks = incoming_blocks.reshape((columns * most_slots,) + kv_cache.shape[1:])
    moved = flat_blocks[own_sources * most_slots + arrival]
    moved = moved.reshape(own_beams, CACHE // PAGE, 2, PAGE, KVH, HD)
    keys = moved[:, :, 0].reshape(own_beams, CACHE, KVH, HD)
    values = moved[:, :, 1].reshape(own_beams, CACHE, KVH, HD)
    positions = lax.dynamic_slice_in_dim(lengths, my_column * own_beams, own_beams)
    query_cols = own_qkv[:, : QH * HD].reshape(own_beams, QH, HD).astype(jnp.float32)
    key_cols = own_qkv[:, QH * HD : (QH + KVH) * HD].reshape(own_beams, KVH, HD).astype(jnp.float32)
    value_new = own_qkv[:, (QH + KVH) * HD :].reshape(own_beams, KVH, HD)
    queries = rotary_embed(query_cols, positions).astype(jnp.bfloat16)
    fresh_key = rotary_embed(key_cols, positions).astype(jnp.bfloat16)
    attn = attend(queries, fresh_key, value_new, keys, values, positions)
    cores = lax.axis_size("c")
    pairs = columns // cores
    pair_feats = attn.reshape(own_beams, pairs, 1, cores * attn.shape[1] // columns)
    doubled = jnp.broadcast_to(pair_feats, (own_beams, pairs, cores, pair_feats.shape[3]))
    head_rows = lax.all_to_all(
        doubled.reshape(own_beams, columns, pair_feats.shape[3]), BEAM, 1, 1, tiled=True
    )
    block = attn.shape[1] // columns
    partial = None
    for half in range(cores):
        term = jnp.einsum(
            "bjh,hpc->jbpc",
            head_rows[:, :, half * block : (half + 1) * block],
            w_pair[half * block : (half + 1) * block],
            preferred_element_type=jnp.float32,
        ).astype(jnp.bfloat16).astype(jnp.float32)
        partial = term if partial is None else partial + term
    partial = partial.astype(jnp.bfloat16).reshape(grouped_row_block, pairs, block)
    spread = lax.all_to_all(partial.transpose(1, 0, 2), PAIR, 0, 0, tiled=True)
    return jnp.sum(spread.astype(jnp.float32), axis=0).astype(jnp.bfloat16)


def solution(mesh):
    sizes = dict(mesh.shape)
    parts = mesh.devices.reshape(4, sizes["owner"] // 4, 2, sizes["beam"] // 4, 2)
    view = Mesh(parts, OWNER + BEAM)
    return jax.shard_map(
        shards,
        mesh=view,
        in_specs=(
            P(OWNER, None),
            P(),
            P(OWNER, BEAM),
            P(BEAM, OWNER),
            P(OWNER + BEAM, None, None, None),
            P(OWNER),
            P(OWNER, None),
            P(OWNER),
        ),
        out_specs=P(OWNER, BEAM),
        check_vma=False,
    )
```

```python
import jax
import jax.numpy as jnp
from jax import lax
from jax.sharding import Mesh
from jax.sharding import PartitionSpec as P

QH = 64
KVH = 8
HD = 128
CACHE = 32
PAGE = 8
QKV = 10240

OWNER = ("x", "yh")
BEAM = ("yl", "z", "c")
PAIR = ("yl", "z")


def rotary_embed(values, positions):
    half = values.shape[-1] // 2
    freqs = 500000.0 ** (-(jnp.arange(half, dtype=jnp.float32) * 2.0) / values.shape[-1])
    angles = positions.astype(jnp.float32)[:, None] * freqs[None, :]
    cosine = jnp.cos(angles)[:, None, :]
    sine = jnp.sin(angles)[:, None, :]
    first = values[..., :half]
    second = values[..., half:]
    return jnp.concatenate(
        [first * cosine - second * sine, second * cosine + first * sine], axis=-1
    )


def regroup(blocks):
    return lax.all_to_all(blocks, BEAM, split_axis=1, concat_axis=1, tiled=True)


def gather_rows(tile, axis, count):
    copies = jnp.broadcast_to(tile[None], (count,) + tile.shape)
    return lax.all_to_all(copies, axis, 0, 0, tiled=True).reshape((-1,) + tile.shape[1:])


def attend(queries, fresh_key, value_new, keys, values, positions):
    beams = queries.shape[0]
    grouped_heads = queries.reshape(beams, KVH, QH // KVH, HD)
    scale_factor = HD ** (-0.5)
    scores = (
        jnp.einsum("bkgd,btkd->bkgt", grouped_heads, keys, preferred_element_type=jnp.float32)
        * scale_factor
    )
    local_beam_score = (
        jnp.einsum("rhap,rhp->rha", grouped_heads, fresh_key, preferred_element_type=jnp.float32)
        * scale_factor
    )
    valid = (jnp.arange(keys.shape[1], dtype=jnp.int32)[None, :] < positions[:, None])[
        :, None, None, :
    ]
    scores = jnp.where(valid, scores, -1e30)
    highest = jnp.maximum(jnp.max(scores, axis=-1), local_beam_score)
    weights = jnp.where(valid, jnp.exp(scores - highest[..., None]), 0.0)
    own_weight = jnp.exp(local_beam_score - highest)
    totals = jnp.sum(weights, axis=-1) + own_weight
    probs = (weights / totals[..., None]).astype(jnp.bfloat16)
    own_prob = (own_weight / totals).astype(jnp.bfloat16)
    output = jnp.einsum("bkgt,btkd->bkgd", probs, values, preferred_element_type=jnp.float32)
    output = (
        output
        + own_prob.astype(jnp.float32)[..., None] * value_new.astype(jnp.float32)[:, :, None, :]
    )
    return output.reshape(beams, QH * HD).astype(jnp.bfloat16)


def shards(hidden, norm_gain, w_qkv, w_out, kv_cache, lengths, kept_parent_device, keep_block):
    columns = lax.axis_size(BEAM)
    my_column = lax.axis_index(BEAM)
    grouped_row_block = hidden.shape[0]
    own_beams = grouped_row_block // columns
    halves = w_out.reshape(w_out.shape[0], lax.axis_size("c"), w_out.shape[1] // lax.axis_size("c"))
    w_local = lax.all_to_all(halves, "c", 1, 0, tiled=True).reshape(-1, halves.shape[2])
    w_pair = lax.all_gather(w_local, OWNER, axis=1, tiled=False)
    floats = hidden.astype(jnp.float32)
    scale_rms = lax.rsqrt(jnp.mean(floats * floats, axis=-1, keepdims=True) + 1e-05)
    normed = (floats * scale_rms * norm_gain.astype(jnp.float32)).astype(jnp.bfloat16)
    stack = gather_rows(w_qkv, "yh", lax.axis_size("yh"))
    xs = lax.axis_size("x")
    assert xs == 4
    me = lax.axis_index("x")
    ahead = [(i, (i + 1) % xs) for i in range(xs)]
    behind = [(i, (i - 1) % xs) for i in range(xs)]
    from_left = lax.ppermute(stack, "x", ahead)
    from_right = lax.ppermute(stack, "x", behind)
    cut = stack.shape[0] // 2
    far = jnp.concatenate(
        [lax.ppermute(from_left[:cut], "x", ahead), lax.ppermute(from_right[cut:], "x", behind)],
        axis=0,
    )
    rows = stack.shape[0]
    projected = None
    for step, piece in ((0, stack), (1, from_right), (3, from_left), (2, far)):
        start = ((me + step) % xs) * rows
        block = lax.dynamic_slice_in_dim(normed, start, rows, axis=1)
        term = jnp.einsum(
            "jbd,dc->bjc",
            block.reshape(columns, own_beams, rows),
            piece,
            preferred_element_type=jnp.float32,
        )
        projected = term if projected is None else projected + term
    own_qkv = regroup(projected.astype(jnp.bfloat16)).reshape(own_beams, QKV)
    blk_dev = kv_cache.shape[0]
    most_slots = max(2, 2 * blk_dev // columns)
    sources = kept_parent_device.reshape(columns, blk_dev)
    picked = keep_block.reshape(columns, blk_dev)
    is_mine = (sources == my_column).astype(jnp.int32)
    ranks = jnp.cumsum(is_mine, axis=1) - 1
    slot_ids = jnp.arange(most_slots, dtype=jnp.int32)
    chosen = is_mine[:, :, None] * (ranks[:, :, None] == slot_ids[None, None, :]).astype(jnp.int32)
    send_table = jnp.sum(chosen * picked[:, :, None], axis=1)
    outgoing = kv_cache[send_table.reshape(-1)].reshape((columns, most_slots) + kv_cache.shape[1:])
    incoming_blocks = lax.all_to_all(outgoing, BEAM, split_axis=0, concat_axis=0, tiled=True)
    own_sources = lax.dynamic_index_in_dim(sources, my_column, 0, keepdims=False)
    one_hot = (own_sources[:, None] == jnp.arange(columns, dtype=jnp.int32)[None, :]).astype(
        jnp.int32
    )
    earlier = jnp.cumsum(one_hot, axis=0) - one_hot
    arrival = jnp.sum(earlier * one_hot, axis=1)
    flat_blocks = incoming_blocks.reshape((columns * most_slots,) + kv_cache.shape[1:])
    moved = flat_blocks[own_sources * most_slots + arrival]
    moved = moved.reshape(own_beams, CACHE // PAGE, 2, PAGE, KVH, HD)
    keys = moved[:, :, 0].reshape(own_beams, CACHE, KVH, HD)
    values = moved[:, :, 1].reshape(own_beams, CACHE, KVH, HD)
    positions = lax.dynamic_slice_in_dim(lengths, my_column * own_beams, own_beams)
    query_cols = own_qkv[:, : QH * HD].reshape(own_beams, QH, HD).astype(jnp.float32)
    key_cols = own_qkv[:, QH * HD : (QH + KVH) * HD].reshape(own_beams, KVH, HD).astype(jnp.float32)
    value_new = own_qkv[:, (QH + KVH) * HD :].reshape(own_beams, KVH, HD)
    queries = rotary_embed(query_cols, positions).astype(jnp.bfloat16)
    fresh_key = rotary_embed(key_cols, positions).astype(jnp.bfloat16)
    attn = attend(queries, fresh_key, value_new, keys, values, positions)
    cores = lax.axis_size("c")
    pairs = columns // cores
    pair_feats = attn.reshape(own_beams, pairs, 1, cores * attn.shape[1] // columns)
    doubled = jnp.broadcast_to(pair_feats, (own_beams, pairs, cores, pair_feats.shape[3]))
    head_rows = lax.all_to_all(
        doubled.reshape(own_beams, columns, pair_feats.shape[3]), BEAM, 1, 1, tiled=True
    )
    block = attn.shape[1] // columns
    partial = None
    for half in range(cores):
        term = jnp.einsum(
            "bjh,hpc->jbpc",
            head_rows[:, :, half * block : (half + 1) * block],
            w_pair[half * block : (half + 1) * block],
            preferred_element_type=jnp.float32,
        ).astype(jnp.bfloat16).astype(jnp.float32)
        partial = term if partial is None else partial + term
    partial = partial.astype(jnp.bfloat16).reshape(grouped_row_block, pairs, block)
    spread = lax.all_to_all(partial.transpose(1, 0, 2), PAIR, 0, 0, tiled=True)
    return jnp.sum(spread.astype(jnp.float32), axis=0).astype(jnp.bfloat16)


def solution(mesh):
    sizes = dict(mesh.shape)
    parts = mesh.devices.reshape(4, sizes["owner"] // 4, 2, sizes["beam"] // 4, 2)
    view = Mesh(parts, OWNER + BEAM)
    return jax.shard_map(
        shards,
        mesh=view,
        in_specs=(
            P(OWNER, None),
            P(),
            P(OWNER, BEAM),
            P(BEAM, OWNER),
            P(OWNER + BEAM, None, None, None),
            P(OWNER),
            P(OWNER, None),
            P(OWNER),
        ),
        out_specs=P(OWNER, BEAM),
        check_vma=False,
    )
```

```python
import jax
import jax.numpy as jnp
from jax import lax
from jax.sharding import Mesh
from jax.sharding import PartitionSpec as P

QH = 64
KVH = 8
HD = 128
CACHE = 32
PAGE = 8
QKV = 10240

OWNER = ("x", "yh")
BEAM = ("yl", "z", "c")
PAIR = ("yl", "z")


def rotary_embed(values, positions):
    half = values.shape[-1] // 2
    freqs = 500000.0 ** (-(jnp.arange(half, dtype=jnp.float32) * 2.0) / values.shape[-1])
    angles = positions.astype(jnp.float32)[:, None] * freqs[None, :]
    cosine = jnp.cos(angles)[:, None, :]
    sine = jnp.sin(angles)[:, None, :]
    first = values[..., :half]
    second = values[..., half:]
    return jnp.concatenate(
        [first * cosine - second * sine, second * cosine + first * sine], axis=-1
    )


def regroup(blocks):
    return lax.all_to_all(blocks, BEAM, split_axis=1, concat_axis=1, tiled=True)


def gather_rows(tile, axis, count):
    copies = jnp.broadcast_to(tile[None], (count,) + tile.shape)
    return lax.all_to_all(copies, axis, 0, 0, tiled=True).reshape((-1,) + tile.shape[1:])


def ring_gather(piece, axis, count):
    ahead = [(i, (i + 1) % count) for i in range(count)]
    behind = [(i, (i - 1) % count) for i in range(count)]
    from_left = lax.ppermute(piece, axis, ahead)
    from_right = lax.ppermute(piece, axis, behind)
    cut = piece.shape[0] // 2
    far = jnp.concatenate(
        [lax.ppermute(from_left[:cut], axis, ahead), lax.ppermute(from_right[cut:], axis, behind)],
        axis=0,
    )
    return [piece, from_right, far, from_left]


def attend(queries, fresh_key, value_new, keys, values, positions):
    beams = queries.shape[0]
    grouped_heads = queries.reshape(beams, KVH, QH // KVH, HD)
    scale_factor = HD ** (-0.5)
    scores = (
        jnp.einsum("bkgd,btkd->bkgt", grouped_heads, keys, preferred_element_type=jnp.float32)
        * scale_factor
    )
    local_beam_score = (
        jnp.einsum("rhap,rhp->rha", grouped_heads, fresh_key, preferred_element_type=jnp.float32)
        * scale_factor
    )
    valid = (jnp.arange(keys.shape[1], dtype=jnp.int32)[None, :] < positions[:, None])[
        :, None, None, :
    ]
    scores = jnp.where(valid, scores, -1e30)
    highest = jnp.maximum(jnp.max(scores, axis=-1), local_beam_score)
    weights = jnp.where(valid, jnp.exp(scores - highest[..., None]), 0.0)
    own_weight = jnp.exp(local_beam_score - highest)
    totals = jnp.sum(weights, axis=-1) + own_weight
    probs = (weights / totals[..., None]).astype(jnp.bfloat16)
    own_prob = (own_weight / totals).astype(jnp.bfloat16)
    output = jnp.einsum("bkgt,btkd->bkgd", probs, values, preferred_element_type=jnp.float32)
    output = (
        output
        + own_prob.astype(jnp.float32)[..., None] * value_new.astype(jnp.float32)[:, :, None, :]
    )
    return output.reshape(beams, QH * HD).astype(jnp.bfloat16)


def shards(hidden, norm_gain, w_qkv, w_out, kv_cache, lengths, kept_parent_device, keep_block):
    columns = lax.axis_size(BEAM)
    my_column = lax.axis_index(BEAM)
    grouped_row_block = hidden.shape[0]
    own_beams = grouped_row_block // columns
    cores = lax.axis_size("c")
    core = lax.axis_index("c")
    halves = w_out.reshape(w_out.shape[0], cores, w_out.shape[1] // cores)
    assert cores == 2
    mine = jnp.take(halves, core, axis=1)
    other = lax.ppermute(jnp.take(halves, 1 - core, axis=1), "c", [(0, 1), (1, 0)])
    w_local = jnp.where(core == 0, jnp.concatenate([mine, other], 0), jnp.concatenate([other, mine], 0))
    w_pair = lax.all_gather(w_local[:, None], OWNER, axis=1, tiled=True)
    floats = hidden.astype(jnp.float32)
    scale_rms = lax.rsqrt(jnp.mean(floats * floats, axis=-1, keepdims=True) + 1e-05)
    normed = (floats * scale_rms * norm_gain.astype(jnp.float32)).astype(jnp.bfloat16)
    xs = lax.axis_size("x")
    ys = lax.axis_size("yh")
    assert xs == 4 and ys == 4
    near = ring_gather(w_qkv, "yh", ys)
    stack = jnp.concatenate(near, axis=0)
    ordered = normed.reshape(normed.shape[0], xs, ys, w_qkv.shape[0])
    ordered = jnp.roll(ordered, -lax.axis_index("x"), axis=1)
    ordered = jnp.roll(ordered, -lax.axis_index("yh"), axis=2)
    ordered = ordered.reshape(columns, own_beams, xs, ys * w_qkv.shape[0])
    rows = stack.shape[0]
    projected = None
    for step, piece in zip((0, 1, 2, 3), ring_gather(stack, "x", xs)):
        term = jnp.einsum(
            "jbd,dc->bjc",
            ordered[:, :, step],
            piece,
            preferred_element_type=jnp.float32,
        )
        projected = term if projected is None else projected + term
    own_qkv = regroup(projected.astype(jnp.bfloat16)).reshape(own_beams, QKV)
    blk_dev = kv_cache.shape[0]
    most_slots = max(2, 2 * blk_dev // columns)
    sources = kept_parent_device.reshape(columns, blk_dev)
    picked = keep_block.reshape(columns, blk_dev)
    is_mine = (sources == my_column).astype(jnp.int32)
    ranks = jnp.cumsum(is_mine, axis=1) - 1
    slot_ids = jnp.arange(most_slots, dtype=jnp.int32)
    chosen = is_mine[:, :, None] * (ranks[:, :, None] == slot_ids[None, None, :]).astype(jnp.int32)
    send_table = jnp.sum(chosen * picked[:, :, None], axis=1)
    outgoing = kv_cache[send_table.reshape(-1)].reshape((columns, most_slots) + kv_cache.shape[1:])
    incoming_blocks = lax.all_to_all(outgoing, BEAM, split_axis=0, concat_axis=0, tiled=True)
    own_sources = lax.dynamic_index_in_dim(sources, my_column, 0, keepdims=False)
    one_hot = (own_sources[:, None] == jnp.arange(columns, dtype=jnp.int32)[None, :]).astype(
        jnp.int32
    )
    earlier = jnp.cumsum(one_hot, axis=0) - one_hot
    arrival = jnp.sum(earlier * one_hot, axis=1)
    flat_blocks = incoming_blocks.reshape((columns * most_slots,) + kv_cache.shape[1:])
    moved = flat_blocks[own_sources * most_slots + arrival]
    moved = moved.reshape(own_beams, CACHE // PAGE, 2, PAGE, KVH, HD)
    keys = moved[:, :, 0].reshape(own_beams, CACHE, KVH, HD)
    values = moved[:, :, 1].reshape(own_beams, CACHE, KVH, HD)
    positions = lax.dynamic_slice_in_dim(lengths, my_column * own_beams, own_beams)
    query_cols = own_qkv[:, : QH * HD].reshape(own_beams, QH, HD).astype(jnp.float32)
    key_cols = own_qkv[:, QH * HD : (QH + KVH) * HD].reshape(own_beams, KVH, HD).astype(jnp.float32)
    value_new = own_qkv[:, (QH + KVH) * HD :].reshape(own_beams, KVH, HD)
    queries = rotary_embed(query_cols, positions).astype(jnp.bfloat16)
    fresh_key = rotary_embed(key_cols, positions).astype(jnp.bfloat16)
    attn = attend(queries, fresh_key, value_new, keys, values, positions)
    pairs = columns // cores
    pair_feats = attn.reshape(own_beams, pairs, 1, cores * attn.shape[1] // columns)
    doubled = jnp.broadcast_to(pair_feats, (own_beams, pairs, cores, pair_feats.shape[3]))
    head_rows = lax.all_to_all(
        doubled.reshape(own_beams, columns, pair_feats.shape[3]), BEAM, 1, 1, tiled=True
    )
    block = attn.shape[1] // columns
    partial = None
    for half in range(cores):
        term = jnp.einsum(
            "bjh,hpc->jbpc",
            head_rows[:, :, half * block : (half + 1) * block],
            w_pair[half * block : (half + 1) * block],
            preferred_element_type=jnp.float32,
        ).astype(jnp.bfloat16).astype(jnp.float32)
        partial = term if partial is None else partial + term
    partial = partial.astype(jnp.bfloat16).reshape(grouped_row_block, pairs, block)
    spread = lax.all_to_all(partial.transpose(1, 0, 2), PAIR, 0, 0, tiled=True)
    return jnp.sum(spread.astype(jnp.float32), axis=0).astype(jnp.bfloat16)


def solution(mesh):
    sizes = dict(mesh.shape)
    parts = mesh.devices.reshape(4, sizes["owner"] // 4, 2, sizes["beam"] // 4, 2)
    view = Mesh(parts, OWNER + BEAM)
    return jax.shard_map(
        shards,
        mesh=view,
        in_specs=(
            P(OWNER, None),
            P(),
            P(OWNER, BEAM),
            P(BEAM, OWNER),
            P(OWNER + BEAM, None, None, None),
            P(OWNER),
            P(OWNER, None),
            P(OWNER),
        ),
        out_specs=P(OWNER, BEAM),
        check_vma=False,
    )
```

```python
import jax
import jax.numpy as jnp
from jax import lax
from jax.sharding import Mesh
from jax.sharding import PartitionSpec as P

QH = 64
KVH = 8
HD = 128
CACHE = 32
PAGE = 8
QKV = 10240

OWNER = ("x", "yh")
BEAM = ("yl", "z", "c")
PAIR = ("yl", "z")


def rotary_embed(values, positions):
    half = values.shape[-1] // 2
    freqs = 500000.0 ** (-(jnp.arange(half, dtype=jnp.float32) * 2.0) / values.shape[-1])
    angles = positions.astype(jnp.float32)[:, None] * freqs[None, :]
    cosine = jnp.cos(angles)[:, None, :]
    sine = jnp.sin(angles)[:, None, :]
    first = values[..., :half]
    second = values[..., half:]
    return jnp.concatenate(
        [first * cosine - second * sine, second * cosine + first * sine], axis=-1
    )


def regroup(blocks):
    return lax.all_to_all(blocks, BEAM, split_axis=1, concat_axis=1, tiled=True)


def gather_rows(tile, axis, count):
    copies = jnp.broadcast_to(tile[None], (count,) + tile.shape)
    return lax.all_to_all(copies, axis, 0, 0, tiled=True).reshape((-1,) + tile.shape[1:])


def attend(queries, fresh_key, value_new, keys, values, positions):
    beams = queries.shape[0]
    grouped_heads = queries.reshape(beams, KVH, QH // KVH, HD)
    scale_factor = HD ** (-0.5)
    scores = (
        jnp.einsum("bkgd,btkd->bkgt", grouped_heads, keys, preferred_element_type=jnp.float32)
        * scale_factor
    )
    local_beam_score = (
        jnp.einsum("rhap,rhp->rha", grouped_heads, fresh_key, preferred_element_type=jnp.float32)
        * scale_factor
    )
    valid = (jnp.arange(keys.shape[1], dtype=jnp.int32)[None, :] < positions[:, None])[
        :, None, None, :
    ]
    scores = jnp.where(valid, scores, -1e30)
    highest = jnp.maximum(jnp.max(scores, axis=-1), local_beam_score)
    weights = jnp.where(valid, jnp.exp(scores - highest[..., None]), 0.0)
    own_weight = jnp.exp(local_beam_score - highest)
    totals = jnp.sum(weights, axis=-1) + own_weight
    probs = (weights / totals[..., None]).astype(jnp.bfloat16)
    own_prob = (own_weight / totals).astype(jnp.bfloat16)
    output = jnp.einsum("bkgt,btkd->bkgd", probs, values, preferred_element_type=jnp.float32)
    output = (
        output
        + own_prob.astype(jnp.float32)[..., None] * value_new.astype(jnp.float32)[:, :, None, :]
    )
    return output.reshape(beams, QH * HD).astype(jnp.bfloat16)


def shards(hidden, norm_gain, w_qkv, w_out, kv_cache, lengths, kept_parent_device, keep_block):
    columns = lax.axis_size(BEAM)
    my_column = lax.axis_index(BEAM)
    grouped_row_block = hidden.shape[0]
    own_beams = grouped_row_block // columns
    cores = lax.axis_size("c")
    core = lax.axis_index("c")
    assert cores == 2
    halves = w_out.reshape(w_out.shape[0], cores, w_out.shape[1] // cores)
    mine = jnp.take(halves, core, axis=1)
    other = lax.ppermute(jnp.take(halves, 1 - core, axis=1), "c", [(0, 1), (1, 0)])
    w_local = jnp.where(core == 0, jnp.concatenate([mine, other], 0), jnp.concatenate([other, mine], 0))
    floats = hidden.astype(jnp.float32)
    scale_rms = lax.rsqrt(jnp.mean(floats * floats, axis=-1, keepdims=True) + 1e-05)
    normed = (floats * scale_rms * norm_gain.astype(jnp.float32)).astype(jnp.bfloat16)
    stack = gather_rows(w_qkv, "yh", lax.axis_size("yh"))
    w_local, stack = lax.optimization_barrier((w_local, stack))
    w_pair = lax.all_gather(w_local[:, None], OWNER, axis=1, tiled=True)
    xs = lax.axis_size("x")
    assert xs == 4
    me = lax.axis_index("x")
    ahead = [(i, (i + 1) % xs) for i in range(xs)]
    behind = [(i, (i - 1) % xs) for i in range(xs)]
    from_left = lax.ppermute(stack, "x", ahead)
    from_right = lax.ppermute(stack, "x", behind)
    cut = stack.shape[0] // 2
    far = jnp.concatenate(
        [lax.ppermute(from_left[:cut], "x", ahead), lax.ppermute(from_right[cut:], "x", behind)],
        axis=0,
    )
    rows = stack.shape[0]
    projected = None
    for step, piece in ((0, stack), (1, from_right), (3, from_left), (2, far)):
        start = ((me + step) % xs) * rows
        block = lax.dynamic_slice_in_dim(normed, start, rows, axis=1)
        term = jnp.einsum(
            "jbd,dc->bjc",
            block.reshape(columns, own_beams, rows),
            piece,
            preferred_element_type=jnp.float32,
        )
        projected = term if projected is None else projected + term
    own_qkv = regroup(projected.astype(jnp.bfloat16)).reshape(own_beams, QKV)
    blk_dev = kv_cache.shape[0]
    most_slots = max(2, 2 * blk_dev // columns)
    sources = kept_parent_device.reshape(columns, blk_dev)
    picked = keep_block.reshape(columns, blk_dev)
    is_mine = (sources == my_column).astype(jnp.int32)
    ranks = jnp.cumsum(is_mine, axis=1) - 1
    slot_ids = jnp.arange(most_slots, dtype=jnp.int32)
    chosen = is_mine[:, :, None] * (ranks[:, :, None] == slot_ids[None, None, :]).astype(jnp.int32)
    send_table = jnp.sum(chosen * picked[:, :, None], axis=1)
    outgoing = kv_cache[send_table.reshape(-1)].reshape((columns, most_slots) + kv_cache.shape[1:])
    incoming_blocks = lax.all_to_all(outgoing, BEAM, split_axis=0, concat_axis=0, tiled=True)
    own_sources = lax.dynamic_index_in_dim(sources, my_column, 0, keepdims=False)
    one_hot = (own_sources[:, None] == jnp.arange(columns, dtype=jnp.int32)[None, :]).astype(
        jnp.int32
    )
    earlier = jnp.cumsum(one_hot, axis=0) - one_hot
    arrival = jnp.sum(earlier * one_hot, axis=1)
    flat_blocks = incoming_blocks.reshape((columns * most_slots,) + kv_cache.shape[1:])
    moved = flat_blocks[own_sources * most_slots + arrival]
    moved = moved.reshape(own_beams, CACHE // PAGE, 2, PAGE, KVH, HD)
    keys = moved[:, :, 0].reshape(own_beams, CACHE, KVH, HD)
    values = moved[:, :, 1].reshape(own_beams, CACHE, KVH, HD)
    positions = lax.dynamic_slice_in_dim(lengths, my_column * own_beams, own_beams)
    query_cols = own_qkv[:, : QH * HD].reshape(own_beams, QH, HD).astype(jnp.float32)
    key_cols = own_qkv[:, QH * HD : (QH + KVH) * HD].reshape(own_beams, KVH, HD).astype(jnp.float32)
    value_new = own_qkv[:, (QH + KVH) * HD :].reshape(own_beams, KVH, HD)
    queries = rotary_embed(query_cols, positions).astype(jnp.bfloat16)
    fresh_key = rotary_embed(key_cols, positions).astype(jnp.bfloat16)
    attn = attend(queries, fresh_key, value_new, keys, values, positions)
    pairs = columns // cores
    pair_feats = attn.reshape(own_beams, pairs, 1, cores * attn.shape[1] // columns)
    doubled = jnp.broadcast_to(pair_feats, (own_beams, pairs, cores, pair_feats.shape[3]))
    head_rows = lax.all_to_all(
        doubled.reshape(own_beams, columns, pair_feats.shape[3]), BEAM, 1, 1, tiled=True
    )
    block = attn.shape[1] // columns
    partial = None
    for half in range(cores):
        term = jnp.einsum(
            "bjh,hpc->jbpc",
            head_rows[:, :, half * block : (half + 1) * block],
            w_pair[half * block : (half + 1) * block],
            preferred_element_type=jnp.float32,
        ).astype(jnp.bfloat16).astype(jnp.float32)
        partial = term if partial is None else partial + term
    partial = partial.astype(jnp.bfloat16).reshape(grouped_row_block, pairs, block)
    spread = lax.all_to_all(partial.transpose(1, 0, 2), PAIR, 0, 0, tiled=True)
    return jnp.sum(spread.astype(jnp.float32), axis=0).astype(jnp.bfloat16)


def solution(mesh):
    sizes = dict(mesh.shape)
    parts = mesh.devices.reshape(4, sizes["owner"] // 4, 2, sizes["beam"] // 4, 2)
    view = Mesh(parts, OWNER + BEAM)
    return jax.shard_map(
        shards,
        mesh=view,
        in_specs=(
            P(OWNER, None),
            P(),
            P(OWNER, BEAM),
            P(BEAM, OWNER),
            P(OWNER + BEAM, None, None, None),
            P(OWNER),
            P(OWNER, None),
            P(OWNER),
        ),
        out_specs=P(OWNER, BEAM),
        check_vma=False,
    )
```

```python
import jax
import jax.numpy as jnp
from jax import lax
from jax.sharding import Mesh
from jax.sharding import PartitionSpec as P

QH = 64
KVH = 8
HD = 128
CACHE = 32
PAGE = 8
QKV = 10240

OWNER = ("x", "yh")
BEAM = ("yl", "z", "c")
PAIR = ("yl", "z")


def rotary_embed(values, positions):
    half = values.shape[-1] // 2
    freqs = 500000.0 ** (-(jnp.arange(half, dtype=jnp.float32) * 2.0) / values.shape[-1])
    angles = positions.astype(jnp.float32)[:, None] * freqs[None, :]
    cosine = jnp.cos(angles)[:, None, :]
    sine = jnp.sin(angles)[:, None, :]
    first = values[..., :half]
    second = values[..., half:]
    return jnp.concatenate(
        [first * cosine - second * sine, second * cosine + first * sine], axis=-1
    )


def regroup(blocks):
    return lax.all_to_all(blocks, BEAM, split_axis=1, concat_axis=1, tiled=True)


def gather_rows(tile, axis, count):
    copies = jnp.broadcast_to(tile[None], (count,) + tile.shape)
    return lax.all_to_all(copies, axis, 0, 0, tiled=True).reshape((-1,) + tile.shape[1:])


def attend(queries, fresh_key, value_new, keys, values, positions):
    beams = queries.shape[0]
    grouped_heads = queries.reshape(beams, KVH, QH // KVH, HD)
    scale_factor = HD ** (-0.5)
    scores = (
        jnp.einsum("bkgd,btkd->bkgt", grouped_heads, keys, preferred_element_type=jnp.float32)
        * scale_factor
    )
    local_beam_score = (
        jnp.einsum("rhap,rhp->rha", grouped_heads, fresh_key, preferred_element_type=jnp.float32)
        * scale_factor
    )
    valid = (jnp.arange(keys.shape[1], dtype=jnp.int32)[None, :] < positions[:, None])[
        :, None, None, :
    ]
    scores = jnp.where(valid, scores, -1e30)
    highest = jnp.maximum(jnp.max(scores, axis=-1), local_beam_score)
    weights = jnp.where(valid, jnp.exp(scores - highest[..., None]), 0.0)
    own_weight = jnp.exp(local_beam_score - highest)
    totals = jnp.sum(weights, axis=-1) + own_weight
    probs = (weights / totals[..., None]).astype(jnp.bfloat16)
    own_prob = (own_weight / totals).astype(jnp.bfloat16)
    output = jnp.einsum("bkgt,btkd->bkgd", probs, values, preferred_element_type=jnp.float32)
    output = (
        output
        + own_prob.astype(jnp.float32)[..., None] * value_new.astype(jnp.float32)[:, :, None, :]
    )
    return output.reshape(beams, QH * HD).astype(jnp.bfloat16)


def shards(hidden, norm_gain, w_qkv, w_out, kv_cache, lengths, kept_parent_device, keep_block):
    columns = lax.axis_size(BEAM)
    my_column = lax.axis_index(BEAM)
    grouped_row_block = hidden.shape[0]
    own_beams = grouped_row_block // columns
    cores = lax.axis_size("c")
    core = lax.axis_index("c")
    assert cores == 2
    halves = w_out.reshape(w_out.shape[0], cores, w_out.shape[1] // cores)
    mine = jnp.take(halves, core, axis=1)
    other = lax.ppermute(jnp.take(halves, 1 - core, axis=1), "c", [(0, 1), (1, 0)])
    w_local = jnp.where(core == 0, jnp.concatenate([mine, other], 0), jnp.concatenate([other, mine], 0))
    floats = hidden.astype(jnp.float32)
    scale_rms = lax.rsqrt(jnp.mean(floats * floats, axis=-1, keepdims=True) + 1e-05)
    normed = (floats * scale_rms * norm_gain.astype(jnp.float32)).astype(jnp.bfloat16)
    stack = gather_rows(w_qkv, "yh", lax.axis_size("yh"))
    xs = lax.axis_size("x")
    assert xs == 4
    me = lax.axis_index("x")
    ahead = [(i, (i + 1) % xs) for i in range(xs)]
    behind = [(i, (i - 1) % xs) for i in range(xs)]
    from_left = lax.ppermute(stack, "x", ahead)
    from_right = lax.ppermute(stack, "x", behind)
    w_local, from_left, from_right = lax.optimization_barrier((w_local, from_left, from_right))
    w_pair = lax.all_gather(w_local[:, None], OWNER, axis=1, tiled=True)
    cut = stack.shape[0] // 2
    far = jnp.concatenate(
        [lax.ppermute(from_left[:cut], "x", ahead), lax.ppermute(from_right[cut:], "x", behind)],
        axis=0,
    )
    rows = stack.shape[0]
    projected = None
    for step, piece in ((0, stack), (1, from_right), (3, from_left), (2, far)):
        start = ((me + step) % xs) * rows
        block = lax.dynamic_slice_in_dim(normed, start, rows, axis=1)
        term = jnp.einsum(
            "jbd,dc->bjc",
            block.reshape(columns, own_beams, rows),
            piece,
            preferred_element_type=jnp.float32,
        )
        projected = term if projected is None else projected + term
    own_qkv = regroup(projected.astype(jnp.bfloat16)).reshape(own_beams, QKV)
    blk_dev = kv_cache.shape[0]
    most_slots = max(2, 2 * blk_dev // columns)
    sources = kept_parent_device.reshape(columns, blk_dev)
    picked = keep_block.reshape(columns, blk_dev)
    is_mine = (sources == my_column).astype(jnp.int32)
    ranks = jnp.cumsum(is_mine, axis=1) - 1
    slot_ids = jnp.arange(most_slots, dtype=jnp.int32)
    chosen = is_mine[:, :, None] * (ranks[:, :, None] == slot_ids[None, None, :]).astype(jnp.int32)
    send_table = jnp.sum(chosen * picked[:, :, None], axis=1)
    outgoing = kv_cache[send_table.reshape(-1)].reshape((columns, most_slots) + kv_cache.shape[1:])
    incoming_blocks = lax.all_to_all(outgoing, BEAM, split_axis=0, concat_axis=0, tiled=True)
    own_sources = lax.dynamic_index_in_dim(sources, my_column, 0, keepdims=False)
    one_hot = (own_sources[:, None] == jnp.arange(columns, dtype=jnp.int32)[None, :]).astype(
        jnp.int32
    )
    earlier = jnp.cumsum(one_hot, axis=0) - one_hot
    arrival = jnp.sum(earlier * one_hot, axis=1)
    flat_blocks = incoming_blocks.reshape((columns * most_slots,) + kv_cache.shape[1:])
    moved = flat_blocks[own_sources * most_slots + arrival]
    moved = moved.reshape(own_beams, CACHE // PAGE, 2, PAGE, KVH, HD)
    keys = moved[:, :, 0].reshape(own_beams, CACHE, KVH, HD)
    values = moved[:, :, 1].reshape(own_beams, CACHE, KVH, HD)
    positions = lax.dynamic_slice_in_dim(lengths, my_column * own_beams, own_beams)
    query_cols = own_qkv[:, : QH * HD].reshape(own_beams, QH, HD).astype(jnp.float32)
    key_cols = own_qkv[:, QH * HD : (QH + KVH) * HD].reshape(own_beams, KVH, HD).astype(jnp.float32)
    value_new = own_qkv[:, (QH + KVH) * HD :].reshape(own_beams, KVH, HD)
    queries = rotary_embed(query_cols, positions).astype(jnp.bfloat16)
    fresh_key = rotary_embed(key_cols, positions).astype(jnp.bfloat16)
    attn = attend(queries, fresh_key, value_new, keys, values, positions)
    pairs = columns // cores
    pair_feats = attn.reshape(own_beams, pairs, 1, cores * attn.shape[1] // columns)
    doubled = jnp.broadcast_to(pair_feats, (own_beams, pairs, cores, pair_feats.shape[3]))
    head_rows = lax.all_to_all(
        doubled.reshape(own_beams, columns, pair_feats.shape[3]), BEAM, 1, 1, tiled=True
    )
    block = attn.shape[1] // columns
    partial = None
    for half in range(cores):
        term = jnp.einsum(
            "bjh,hpc->jbpc",
            head_rows[:, :, half * block : (half + 1) * block],
            w_pair[half * block : (half + 1) * block],
            preferred_element_type=jnp.float32,
        ).astype(jnp.bfloat16).astype(jnp.float32)
        partial = term if partial is None else partial + term
    partial = partial.astype(jnp.bfloat16).reshape(grouped_row_block, pairs, block)
    spread = lax.all_to_all(partial.transpose(1, 0, 2), PAIR, 0, 0, tiled=True)
    return jnp.sum(spread.astype(jnp.float32), axis=0).astype(jnp.bfloat16)


def solution(mesh):
    sizes = dict(mesh.shape)
    parts = mesh.devices.reshape(4, sizes["owner"] // 4, 2, sizes["beam"] // 4, 2)
    view = Mesh(parts, OWNER + BEAM)
    return jax.shard_map(
        shards,
        mesh=view,
        in_specs=(
            P(OWNER, None),
            P(),
            P(OWNER, BEAM),
            P(BEAM, OWNER),
            P(OWNER + BEAM, None, None, None),
            P(OWNER),
            P(OWNER, None),
            P(OWNER),
        ),
        out_specs=P(OWNER, BEAM),
        check_vma=False,
    )
```

```python
import jax
import jax.numpy as jnp
from jax import lax
from jax.sharding import Mesh
from jax.sharding import PartitionSpec as P

QH = 64
KVH = 8
HD = 128
CACHE = 32
PAGE = 8
QKV = 10240

OWNER = ("x", "yh")
BEAM = ("yl", "z", "c")
PAIR = ("yl", "z")


def rotary_embed(values, positions):
    half = values.shape[-1] // 2
    freqs = 500000.0 ** (-(jnp.arange(half, dtype=jnp.float32) * 2.0) / values.shape[-1])
    angles = positions.astype(jnp.float32)[:, None] * freqs[None, :]
    cosine = jnp.cos(angles)[:, None, :]
    sine = jnp.sin(angles)[:, None, :]
    first = values[..., :half]
    second = values[..., half:]
    return jnp.concatenate(
        [first * cosine - second * sine, second * cosine + first * sine], axis=-1
    )


def regroup(blocks):
    return lax.all_to_all(blocks, BEAM, split_axis=1, concat_axis=1, tiled=True)


def gather_rows(tile, axis, count):
    copies = jnp.broadcast_to(tile[None], (count,) + tile.shape)
    return lax.all_to_all(copies, axis, 0, 0, tiled=True).reshape((-1,) + tile.shape[1:])


def ring_near(piece, axis, count):
    ahead = [(i, (i + 1) % count) for i in range(count)]
    behind = [(i, (i - 1) % count) for i in range(count)]
    return lax.ppermute(piece, axis, ahead), lax.ppermute(piece, axis, behind)


def ring_far(piece, near, axis, count):
    ahead = [(i, (i + 1) % count) for i in range(count)]
    behind = [(i, (i - 1) % count) for i in range(count)]
    from_left, from_right = near
    cut = piece.shape[0] // 2
    far = jnp.concatenate(
        [lax.ppermute(from_left[:cut], axis, ahead), lax.ppermute(from_right[cut:], axis, behind)],
        axis=0,
    )
    return [piece, from_right, far, from_left]


def attend(queries, fresh_key, value_new, keys, values, positions):
    beams = queries.shape[0]
    grouped_heads = queries.reshape(beams, KVH, QH // KVH, HD)
    scale_factor = HD ** (-0.5)
    scores = (
        jnp.einsum("bkgd,btkd->bkgt", grouped_heads, keys, preferred_element_type=jnp.float32)
        * scale_factor
    )
    local_beam_score = (
        jnp.einsum("rhap,rhp->rha", grouped_heads, fresh_key, preferred_element_type=jnp.float32)
        * scale_factor
    )
    valid = (jnp.arange(keys.shape[1], dtype=jnp.int32)[None, :] < positions[:, None])[
        :, None, None, :
    ]
    scores = jnp.where(valid, scores, -1e30)
    highest = jnp.maximum(jnp.max(scores, axis=-1), local_beam_score)
    weights = jnp.where(valid, jnp.exp(scores - highest[..., None]), 0.0)
    own_weight = jnp.exp(local_beam_score - highest)
    totals = jnp.sum(weights, axis=-1) + own_weight
    probs = (weights / totals[..., None]).astype(jnp.bfloat16)
    own_prob = (own_weight / totals).astype(jnp.bfloat16)
    output = jnp.einsum("bkgt,btkd->bkgd", probs, values, preferred_element_type=jnp.float32)
    output = (
        output
        + own_prob.astype(jnp.float32)[..., None] * value_new.astype(jnp.float32)[:, :, None, :]
    )
    return output.reshape(beams, QH * HD).astype(jnp.bfloat16)


def shards(hidden, norm_gain, w_qkv, w_out, kv_cache, lengths, kept_parent_device, keep_block):
    columns = lax.axis_size(BEAM)
    my_column = lax.axis_index(BEAM)
    grouped_row_block = hidden.shape[0]
    own_beams = grouped_row_block // columns
    cores = lax.axis_size("c")
    core = lax.axis_index("c")
    assert cores == 2
    halves = w_out.reshape(w_out.shape[0], cores, w_out.shape[1] // cores)
    mine = jnp.take(halves, core, axis=1)
    other = lax.ppermute(jnp.take(halves, 1 - core, axis=1), "c", [(0, 1), (1, 0)])
    w_local = jnp.where(core == 0, jnp.concatenate([mine, other], 0), jnp.concatenate([other, mine], 0))
    floats = hidden.astype(jnp.float32)
    scale_rms = lax.rsqrt(jnp.mean(floats * floats, axis=-1, keepdims=True) + 1e-05)
    normed = (floats * scale_rms * norm_gain.astype(jnp.float32)).astype(jnp.bfloat16)
    xs = lax.axis_size("x")
    ys = lax.axis_size("yh")
    assert xs == 4 and ys == 4
    me = lax.axis_index("x")
    mine_y = lax.axis_index("yh")
    rows = w_qkv.shape[0]
    wide = 192
    stack = gather_rows(w_qkv[:, :wide], "yh", ys)
    by_x = ring_near(w_qkv[:, wide:], "x", xs)
    near = ring_near(stack, "x", xs)
    w_local, near, by_x = lax.optimization_barrier((w_local, near, by_x))
    w_pair = lax.all_gather(w_local[:, None], OWNER, axis=1, tiled=True)
    stack_b = jnp.concatenate(ring_far(w_qkv[:, wide:], by_x, "x", xs), axis=0)
    pieces_b = ring_far(stack_b, ring_near(stack_b, "yh", ys), "yh", ys)
    pieces_a = ring_far(stack, near, "x", xs)
    part_a = None
    for step, piece in enumerate(pieces_a):
        start = ((me + step) % xs) * ys * rows
        block = lax.dynamic_slice_in_dim(normed, start, ys * rows, axis=1)
        term = jnp.einsum(
            "jbd,dc->bjc",
            block.reshape(columns, own_beams, ys * rows),
            piece,
            preferred_element_type=jnp.float32,
        )
        part_a = term if part_a is None else part_a + term
    part_b = None
    for step, piece in enumerate(pieces_b):
        block = jnp.concatenate(
            [
                lax.dynamic_slice_in_dim(
                    normed, (((me + dx) % xs) * ys + (mine_y + step) % ys) * rows, rows, axis=1
                )
                for dx in range(xs)
            ],
            axis=1,
        )
        term = jnp.einsum(
            "jbd,dc->bjc",
            block.reshape(columns, own_beams, xs * rows),
            piece,
            preferred_element_type=jnp.float32,
        )
        part_b = term if part_b is None else part_b + term
    projected = jnp.concatenate([part_a, part_b], axis=-1)
    own_qkv = regroup(projected.astype(jnp.bfloat16)).reshape(own_beams, QKV)
    blk_dev = kv_cache.shape[0]
    most_slots = max(2, 2 * blk_dev // columns)
    sources = kept_parent_device.reshape(columns, blk_dev)
    picked = keep_block.reshape(columns, blk_dev)
    is_mine = (sources == my_column).astype(jnp.int32)
    ranks = jnp.cumsum(is_mine, axis=1) - 1
    slot_ids = jnp.arange(most_slots, dtype=jnp.int32)
    chosen = is_mine[:, :, None] * (ranks[:, :, None] == slot_ids[None, None, :]).astype(jnp.int32)
    send_table = jnp.sum(chosen * picked[:, :, None], axis=1)
    outgoing = kv_cache[send_table.reshape(-1)].reshape((columns, most_slots) + kv_cache.shape[1:])
    incoming_blocks = lax.all_to_all(outgoing, BEAM, split_axis=0, concat_axis=0, tiled=True)
    own_sources = lax.dynamic_index_in_dim(sources, my_column, 0, keepdims=False)
    one_hot = (own_sources[:, None] == jnp.arange(columns, dtype=jnp.int32)[None, :]).astype(
        jnp.int32
    )
    earlier = jnp.cumsum(one_hot, axis=0) - one_hot
    arrival = jnp.sum(earlier * one_hot, axis=1)
    flat_blocks = incoming_blocks.reshape((columns * most_slots,) + kv_cache.shape[1:])
    moved = flat_blocks[own_sources * most_slots + arrival]
    moved = moved.reshape(own_beams, CACHE // PAGE, 2, PAGE, KVH, HD)
    keys = moved[:, :, 0].reshape(own_beams, CACHE, KVH, HD)
    values = moved[:, :, 1].reshape(own_beams, CACHE, KVH, HD)
    positions = lax.dynamic_slice_in_dim(lengths, my_column * own_beams, own_beams)
    query_cols = own_qkv[:, : QH * HD].reshape(own_beams, QH, HD).astype(jnp.float32)
    key_cols = own_qkv[:, QH * HD : (QH + KVH) * HD].reshape(own_beams, KVH, HD).astype(jnp.float32)
    value_new = own_qkv[:, (QH + KVH) * HD :].reshape(own_beams, KVH, HD)
    queries = rotary_embed(query_cols, positions).astype(jnp.bfloat16)
    fresh_key = rotary_embed(key_cols, positions).astype(jnp.bfloat16)
    attn = attend(queries, fresh_key, value_new, keys, values, positions)
    pairs = columns // cores
    pair_feats = attn.reshape(own_beams, pairs, 1, cores * attn.shape[1] // columns)
    doubled = jnp.broadcast_to(pair_feats, (own_beams, pairs, cores, pair_feats.shape[3]))
    head_rows = lax.all_to_all(
        doubled.reshape(own_beams, columns, pair_feats.shape[3]), BEAM, 1, 1, tiled=True
    )
    block = attn.shape[1] // columns
    partial = None
    for half in range(cores):
        term = jnp.einsum(
            "bjh,hpc->jbpc",
            head_rows[:, :, half * block : (half + 1) * block],
            w_pair[half * block : (half + 1) * block],
            preferred_element_type=jnp.float32,
        ).astype(jnp.bfloat16).astype(jnp.float32)
        partial = term if partial is None else partial + term
    partial = partial.astype(jnp.bfloat16).reshape(grouped_row_block, pairs, block)
    spread = lax.all_to_all(partial.transpose(1, 0, 2), PAIR, 0, 0, tiled=True)
    return jnp.sum(spread.astype(jnp.float32), axis=0).astype(jnp.bfloat16)


def solution(mesh):
    sizes = dict(mesh.shape)
    parts = mesh.devices.reshape(4, sizes["owner"] // 4, 2, sizes["beam"] // 4, 2)
    view = Mesh(parts, OWNER + BEAM)
    return jax.shard_map(
        shards,
        mesh=view,
        in_specs=(
            P(OWNER, None),
            P(),
            P(OWNER, BEAM),
            P(BEAM, OWNER),
            P(OWNER + BEAM, None, None, None),
            P(OWNER),
            P(OWNER, None),
            P(OWNER),
        ),
        out_specs=P(OWNER, BEAM),
        check_vma=False,
    )
```

```python
import jax
import jax.numpy as jnp
from jax import lax
from jax.sharding import Mesh
from jax.sharding import PartitionSpec as P

QH = 64
KVH = 8
HD = 128
CACHE = 32
PAGE = 8
QKV = 10240

OWNER = ("x", "yh")
BEAM = ("yl", "z", "c")
PAIR = ("yl", "z")


def rotary_embed(values, positions):
    half = values.shape[-1] // 2
    freqs = 500000.0 ** (-(jnp.arange(half, dtype=jnp.float32) * 2.0) / values.shape[-1])
    angles = positions.astype(jnp.float32)[:, None] * freqs[None, :]
    cosine = jnp.cos(angles)[:, None, :]
    sine = jnp.sin(angles)[:, None, :]
    first = values[..., :half]
    second = values[..., half:]
    return jnp.concatenate(
        [first * cosine - second * sine, second * cosine + first * sine], axis=-1
    )


def regroup(blocks):
    return lax.all_to_all(blocks, BEAM, split_axis=1, concat_axis=1, tiled=True)


def gather_rows(tile, axis, count):
    copies = jnp.broadcast_to(tile[None], (count,) + tile.shape)
    return lax.all_to_all(copies, axis, 0, 0, tiled=True).reshape((-1,) + tile.shape[1:])


def attend(queries, fresh_key, value_new, keys, values, positions):
    beams = queries.shape[0]
    grouped_heads = queries.reshape(beams, KVH, QH // KVH, HD)
    scale_factor = HD ** (-0.5)
    scores = (
        jnp.einsum("bkgd,btkd->bkgt", grouped_heads, keys, preferred_element_type=jnp.float32)
        * scale_factor
    )
    local_beam_score = (
        jnp.einsum("rhap,rhp->rha", grouped_heads, fresh_key, preferred_element_type=jnp.float32)
        * scale_factor
    )
    valid = (jnp.arange(keys.shape[1], dtype=jnp.int32)[None, :] < positions[:, None])[
        :, None, None, :
    ]
    scores = jnp.where(valid, scores, -1e30)
    highest = jnp.maximum(jnp.max(scores, axis=-1), local_beam_score)
    weights = jnp.where(valid, jnp.exp(scores - highest[..., None]), 0.0)
    own_weight = jnp.exp(local_beam_score - highest)
    totals = jnp.sum(weights, axis=-1) + own_weight
    probs = (weights / totals[..., None]).astype(jnp.bfloat16)
    own_prob = (own_weight / totals).astype(jnp.bfloat16)
    output = jnp.einsum("bkgt,btkd->bkgd", probs, values, preferred_element_type=jnp.float32)
    output = (
        output
        + own_prob.astype(jnp.float32)[..., None] * value_new.astype(jnp.float32)[:, :, None, :]
    )
    return output.reshape(beams, QH * HD).astype(jnp.bfloat16)


def shards(hidden, norm_gain, w_qkv, w_out, kv_cache, lengths, kept_parent_device, keep_block):
    columns = lax.axis_size(BEAM)
    my_column = lax.axis_index(BEAM)
    grouped_row_block = hidden.shape[0]
    own_beams = grouped_row_block // columns
    cores = lax.axis_size("c")
    core = lax.axis_index("c")
    assert cores == 2
    halves = w_out.reshape(w_out.shape[0], cores, w_out.shape[1] // cores)
    mine = jnp.take(halves, core, axis=1)
    other = lax.ppermute(jnp.take(halves, 1 - core, axis=1), "c", [(0, 1), (1, 0)])
    w_local = jnp.where(core == 0, jnp.concatenate([mine, other], 0), jnp.concatenate([other, mine], 0))
    floats = hidden.astype(jnp.float32)
    scale_rms = lax.rsqrt(jnp.mean(floats * floats, axis=-1, keepdims=True) + 1e-05)
    normed = (floats * scale_rms * norm_gain.astype(jnp.float32)).astype(jnp.bfloat16)
    blk_dev = kv_cache.shape[0]
    most_slots = max(2, 2 * blk_dev // columns)
    sources = kept_parent_device.reshape(columns, blk_dev)
    picked = keep_block.reshape(columns, blk_dev)
    is_mine = (sources == my_column).astype(jnp.int32)
    ranks = jnp.cumsum(is_mine, axis=1) - 1
    slot_ids = jnp.arange(most_slots, dtype=jnp.int32)
    chosen = is_mine[:, :, None] * (ranks[:, :, None] == slot_ids[None, None, :]).astype(jnp.int32)
    send_table = jnp.sum(chosen * picked[:, :, None], axis=1)
    outgoing = kv_cache[send_table.reshape(-1)].reshape((columns, most_slots) + kv_cache.shape[1:])
    incoming_blocks = lax.all_to_all(outgoing, BEAM, split_axis=0, concat_axis=0, tiled=True)
    stack = gather_rows(w_qkv, "yh", lax.axis_size("yh"))
    xs = lax.axis_size("x")
    assert xs == 4
    me = lax.axis_index("x")
    ahead = [(i, (i + 1) % xs) for i in range(xs)]
    behind = [(i, (i - 1) % xs) for i in range(xs)]
    cut = stack.shape[0] // 2
    left_top = lax.ppermute(stack[:cut], "x", ahead)
    left_low = lax.ppermute(stack[cut:], "x", ahead)
    right_top = lax.ppermute(stack[:cut], "x", behind)
    right_low = lax.ppermute(stack[cut:], "x", behind)
    w_local, left_top, right_low = lax.optimization_barrier((w_local, left_top, right_low))
    w_pair = lax.all_gather(w_local[:, None], OWNER, axis=1, tiled=True)
    far_top = lax.ppermute(left_top, "x", ahead)
    far_low = lax.ppermute(right_low, "x", behind)
    incoming_blocks, far_top, far_low = lax.optimization_barrier((incoming_blocks, far_top, far_low))
    from_left = jnp.concatenate([left_top, left_low], axis=0)
    from_right = jnp.concatenate([right_top, right_low], axis=0)
    far = jnp.concatenate([far_top, far_low], axis=0)
    rows = stack.shape[0]
    projected = None
    for step, piece in ((0, stack), (1, from_right), (3, from_left), (2, far)):
        start = ((me + step) % xs) * rows
        block = lax.dynamic_slice_in_dim(normed, start, rows, axis=1)
        term = jnp.einsum(
            "jbd,dc->bjc",
            block.reshape(columns, own_beams, rows),
            piece,
            preferred_element_type=jnp.float32,
        )
        projected = term if projected is None else projected + term
    own_qkv = regroup(projected.astype(jnp.bfloat16)).reshape(own_beams, QKV)
    own_sources = lax.dynamic_index_in_dim(sources, my_column, 0, keepdims=False)
    one_hot = (own_sources[:, None] == jnp.arange(columns, dtype=jnp.int32)[None, :]).astype(
        jnp.int32
    )
    earlier = jnp.cumsum(one_hot, axis=0) - one_hot
    arrival = jnp.sum(earlier * one_hot, axis=1)
    flat_blocks = incoming_blocks.reshape((columns * most_slots,) + kv_cache.shape[1:])
    moved = flat_blocks[own_sources * most_slots + arrival]
    moved = moved.reshape(own_beams, CACHE // PAGE, 2, PAGE, KVH, HD)
    keys = moved[:, :, 0].reshape(own_beams, CACHE, KVH, HD)
    values = moved[:, :, 1].reshape(own_beams, CACHE, KVH, HD)
    positions = lax.dynamic_slice_in_dim(lengths, my_column * own_beams, own_beams)
    query_cols = own_qkv[:, : QH * HD].reshape(own_beams, QH, HD).astype(jnp.float32)
    key_cols = own_qkv[:, QH * HD : (QH + KVH) * HD].reshape(own_beams, KVH, HD).astype(jnp.float32)
    value_new = own_qkv[:, (QH + KVH) * HD :].reshape(own_beams, KVH, HD)
    queries = rotary_embed(query_cols, positions).astype(jnp.bfloat16)
    fresh_key = rotary_embed(key_cols, positions).astype(jnp.bfloat16)
    attn = attend(queries, fresh_key, value_new, keys, values, positions)
    pairs = columns // cores
    pair_feats = attn.reshape(own_beams, pairs, 1, cores * attn.shape[1] // columns)
    doubled = jnp.broadcast_to(pair_feats, (own_beams, pairs, cores, pair_feats.shape[3]))
    head_rows = lax.all_to_all(
        doubled.reshape(own_beams, columns, pair_feats.shape[3]), BEAM, 1, 1, tiled=True
    )
    block = attn.shape[1] // columns
    partial = None
    for half in range(cores):
        term = jnp.einsum(
            "bjh,hpc->jbpc",
            head_rows[:, :, half * block : (half + 1) * block],
            w_pair[half * block : (half + 1) * block],
            preferred_element_type=jnp.float32,
        ).astype(jnp.bfloat16).astype(jnp.float32)
        partial = term if partial is None else partial + term
    partial = partial.astype(jnp.bfloat16).reshape(grouped_row_block, pairs, block)
    spread = lax.all_to_all(partial.transpose(1, 0, 2), PAIR, 0, 0, tiled=True)
    return jnp.sum(spread.astype(jnp.float32), axis=0).astype(jnp.bfloat16)


def solution(mesh):
    sizes = dict(mesh.shape)
    parts = mesh.devices.reshape(4, sizes["owner"] // 4, 2, sizes["beam"] // 4, 2)
    view = Mesh(parts, OWNER + BEAM)
    return jax.shard_map(
        shards,
        mesh=view,
        in_specs=(
            P(OWNER, None),
            P(),
            P(OWNER, BEAM),
            P(BEAM, OWNER),
            P(OWNER + BEAM, None, None, None),
            P(OWNER),
            P(OWNER, None),
            P(OWNER),
        ),
        out_specs=P(OWNER, BEAM),
        check_vma=False,
    )
```

```python
import jax
import jax.numpy as jnp
from jax import lax
from jax.sharding import Mesh
from jax.sharding import PartitionSpec as P

QH = 64
KVH = 8
HD = 128
CACHE = 32
PAGE = 8
QKV = 10240

OWNER = ("x", "yh")
BEAM = ("yl", "z", "c")
PAIR = ("yl", "z")


def rotary_embed(values, positions):
    half = values.shape[-1] // 2
    freqs = 500000.0 ** (-(jnp.arange(half, dtype=jnp.float32) * 2.0) / values.shape[-1])
    angles = positions.astype(jnp.float32)[:, None] * freqs[None, :]
    cosine = jnp.cos(angles)[:, None, :]
    sine = jnp.sin(angles)[:, None, :]
    first = values[..., :half]
    second = values[..., half:]
    return jnp.concatenate(
        [first * cosine - second * sine, second * cosine + first * sine], axis=-1
    )


def regroup(blocks):
    return lax.all_to_all(blocks, BEAM, split_axis=1, concat_axis=1, tiled=True)


def gather_rows(tile, axis, count):
    copies = jnp.broadcast_to(tile[None], (count,) + tile.shape)
    return lax.all_to_all(copies, axis, 0, 0, tiled=True).reshape((-1,) + tile.shape[1:])


def place_ring(piece, axis, inner):
    count = lax.axis_size(axis)
    me = lax.axis_index(axis)
    source = piece if inner is None else inner
    ahead = [(i, (i + 1) % count) for i in range(count)]
    behind = [(i, (i - 1) % count) for i in range(count)]
    from_left = lax.ppermute(source, axis, ahead)
    from_right = lax.ppermute(source, axis, behind)
    cut = source.shape[0] // 2
    far = jnp.concatenate(
        [lax.ppermute(from_left[:cut], axis, ahead), lax.ppermute(from_right[cut:], axis, behind)],
        axis=0,
    )
    placed = jnp.zeros((count,) + source.shape, source.dtype)
    for step, part in ((0, source), (1, from_right), (2, far), (3, from_left)):
        where = ((me + step) % count,) + (0,) * source.ndim
        placed = lax.dynamic_update_slice(placed, part[None], where)
    if inner is None:
        return placed
    return placed.reshape((-1,) + source.shape[1:])


def attend(queries, fresh_key, value_new, keys, values, positions):
    beams = queries.shape[0]
    grouped_heads = queries.reshape(beams, KVH, QH // KVH, HD)
    scale_factor = HD ** (-0.5)
    scores = (
        jnp.einsum("bkgd,btkd->bkgt", grouped_heads, keys, preferred_element_type=jnp.float32)
        * scale_factor
    )
    local_beam_score = (
        jnp.einsum("rhap,rhp->rha", grouped_heads, fresh_key, preferred_element_type=jnp.float32)
        * scale_factor
    )
    valid = (jnp.arange(keys.shape[1], dtype=jnp.int32)[None, :] < positions[:, None])[
        :, None, None, :
    ]
    scores = jnp.where(valid, scores, -1e30)
    highest = jnp.maximum(jnp.max(scores, axis=-1), local_beam_score)
    weights = jnp.where(valid, jnp.exp(scores - highest[..., None]), 0.0)
    own_weight = jnp.exp(local_beam_score - highest)
    totals = jnp.sum(weights, axis=-1) + own_weight
    probs = (weights / totals[..., None]).astype(jnp.bfloat16)
    own_prob = (own_weight / totals).astype(jnp.bfloat16)
    output = jnp.einsum("bkgt,btkd->bkgd", probs, values, preferred_element_type=jnp.float32)
    output = (
        output
        + own_prob.astype(jnp.float32)[..., None] * value_new.astype(jnp.float32)[:, :, None, :]
    )
    return output.reshape(beams, QH * HD).astype(jnp.bfloat16)


def shards(hidden, norm_gain, w_qkv, w_out, kv_cache, lengths, kept_parent_device, keep_block):
    columns = lax.axis_size(BEAM)
    my_column = lax.axis_index(BEAM)
    grouped_row_block = hidden.shape[0]
    own_beams = grouped_row_block // columns
    cores = lax.axis_size("c")
    core = lax.axis_index("c")
    assert cores == 2
    halves = w_out.reshape(w_out.shape[0], cores, w_out.shape[1] // cores)
    mine = jnp.take(halves, core, axis=1)
    other = lax.ppermute(jnp.take(halves, 1 - core, axis=1), "c", [(0, 1), (1, 0)])
    w_local = jnp.where(core == 0, jnp.concatenate([mine, other], 0), jnp.concatenate([other, mine], 0))
    floats = hidden.astype(jnp.float32)
    scale_rms = lax.rsqrt(jnp.mean(floats * floats, axis=-1, keepdims=True) + 1e-05)
    normed = (floats * scale_rms * norm_gain.astype(jnp.float32)).astype(jnp.bfloat16)
    stack = gather_rows(w_qkv, "yh", lax.axis_size("yh"))
    xs = lax.axis_size("x")
    assert xs == 4
    me = lax.axis_index("x")
    ahead = [(i, (i + 1) % xs) for i in range(xs)]
    behind = [(i, (i - 1) % xs) for i in range(xs)]
    from_left = lax.ppermute(stack, "x", ahead)
    from_right = lax.ppermute(stack, "x", behind)
    w_local, from_left, from_right = lax.optimization_barrier((w_local, from_left, from_right))
    w_blocks = place_ring(w_local, "x", place_ring(w_local, "yh", None))
    cut = stack.shape[0] // 2
    far = jnp.concatenate(
        [lax.ppermute(from_left[:cut], "x", ahead), lax.ppermute(from_right[cut:], "x", behind)],
        axis=0,
    )
    rows = stack.shape[0]
    projected = None
    for step, piece in ((0, stack), (1, from_right), (3, from_left), (2, far)):
        start = ((me + step) % xs) * rows
        block = lax.dynamic_slice_in_dim(normed, start, rows, axis=1)
        term = jnp.einsum(
            "jbd,dc->bjc",
            block.reshape(columns, own_beams, rows),
            piece,
            preferred_element_type=jnp.float32,
        )
        projected = term if projected is None else projected + term
    own_qkv = regroup(projected.astype(jnp.bfloat16)).reshape(own_beams, QKV)
    blk_dev = kv_cache.shape[0]
    most_slots = max(2, 2 * blk_dev // columns)
    sources = kept_parent_device.reshape(columns, blk_dev)
    picked = keep_block.reshape(columns, blk_dev)
    is_mine = (sources == my_column).astype(jnp.int32)
    ranks = jnp.cumsum(is_mine, axis=1) - 1
    slot_ids = jnp.arange(most_slots, dtype=jnp.int32)
    chosen = is_mine[:, :, None] * (ranks[:, :, None] == slot_ids[None, None, :]).astype(jnp.int32)
    send_table = jnp.sum(chosen * picked[:, :, None], axis=1)
    outgoing = kv_cache[send_table.reshape(-1)].reshape((columns, most_slots) + kv_cache.shape[1:])
    incoming_blocks = lax.all_to_all(outgoing, BEAM, split_axis=0, concat_axis=0, tiled=True)
    own_sources = lax.dynamic_index_in_dim(sources, my_column, 0, keepdims=False)
    one_hot = (own_sources[:, None] == jnp.arange(columns, dtype=jnp.int32)[None, :]).astype(
        jnp.int32
    )
    earlier = jnp.cumsum(one_hot, axis=0) - one_hot
    arrival = jnp.sum(earlier * one_hot, axis=1)
    flat_blocks = incoming_blocks.reshape((columns * most_slots,) + kv_cache.shape[1:])
    moved = flat_blocks[own_sources * most_slots + arrival]
    moved = moved.reshape(own_beams, CACHE // PAGE, 2, PAGE, KVH, HD)
    keys = moved[:, :, 0].reshape(own_beams, CACHE, KVH, HD)
    values = moved[:, :, 1].reshape(own_beams, CACHE, KVH, HD)
    positions = lax.dynamic_slice_in_dim(lengths, my_column * own_beams, own_beams)
    query_cols = own_qkv[:, : QH * HD].reshape(own_beams, QH, HD).astype(jnp.float32)
    key_cols = own_qkv[:, QH * HD : (QH + KVH) * HD].reshape(own_beams, KVH, HD).astype(jnp.float32)
    value_new = own_qkv[:, (QH + KVH) * HD :].reshape(own_beams, KVH, HD)
    queries = rotary_embed(query_cols, positions).astype(jnp.bfloat16)
    fresh_key = rotary_embed(key_cols, positions).astype(jnp.bfloat16)
    attn = attend(queries, fresh_key, value_new, keys, values, positions)
    pairs = columns // cores
    pair_feats = attn.reshape(own_beams, pairs, 1, cores * attn.shape[1] // columns)
    doubled = jnp.broadcast_to(pair_feats, (own_beams, pairs, cores, pair_feats.shape[3]))
    head_rows = lax.all_to_all(
        doubled.reshape(own_beams, columns, pair_feats.shape[3]), BEAM, 1, 1, tiled=True
    )
    block = attn.shape[1] // columns
    partial = None
    for half in range(cores):
        term = jnp.einsum(
            "bjh,phc->jbpc",
            head_rows[:, :, half * block : (half + 1) * block],
            w_blocks[:, half * block : (half + 1) * block],
            preferred_element_type=jnp.float32,
        ).astype(jnp.bfloat16).astype(jnp.float32)
        partial = term if partial is None else partial + term
    partial = partial.astype(jnp.bfloat16).reshape(grouped_row_block, pairs, block)
    spread = lax.all_to_all(partial.transpose(1, 0, 2), PAIR, 0, 0, tiled=True)
    return jnp.sum(spread.astype(jnp.float32), axis=0).astype(jnp.bfloat16)


def solution(mesh):
    sizes = dict(mesh.shape)
    parts = mesh.devices.reshape(4, sizes["owner"] // 4, 2, sizes["beam"] // 4, 2)
    view = Mesh(parts, OWNER + BEAM)
    return jax.shard_map(
        shards,
        mesh=view,
        in_specs=(
            P(OWNER, None),
            P(),
            P(OWNER, BEAM),
            P(BEAM, OWNER),
            P(OWNER + BEAM, None, None, None),
            P(OWNER),
            P(OWNER, None),
            P(OWNER),
        ),
        out_specs=P(OWNER, BEAM),
        check_vma=False,
    )
```

```python
import jax
import jax.numpy as jnp
from jax import lax
from jax.sharding import Mesh
from jax.sharding import PartitionSpec as P

QH = 64
KVH = 8
HD = 128
CACHE = 32
PAGE = 8
QKV = 10240

OWNER = ("x", "yh")
BEAM = ("yl", "z", "c")
PAIR = ("yl", "z")


def rotary_embed(values, positions):
    half = values.shape[-1] // 2
    freqs = 500000.0 ** (-(jnp.arange(half, dtype=jnp.float32) * 2.0) / values.shape[-1])
    angles = positions.astype(jnp.float32)[:, None] * freqs[None, :]
    cosine = jnp.cos(angles)[:, None, :]
    sine = jnp.sin(angles)[:, None, :]
    first = values[..., :half]
    second = values[..., half:]
    return jnp.concatenate(
        [first * cosine - second * sine, second * cosine + first * sine], axis=-1
    )


def regroup(blocks):
    return lax.all_to_all(blocks, BEAM, split_axis=1, concat_axis=1, tiled=True)


def gather_rows(tile, axis, count):
    copies = jnp.broadcast_to(tile[None], (count,) + tile.shape)
    return lax.all_to_all(copies, axis, 0, 0, tiled=True).reshape((-1,) + tile.shape[1:])


def place_ring(piece, axis, inner):
    count = lax.axis_size(axis)
    me = lax.axis_index(axis)
    source = piece if inner is None else inner
    ahead = [(i, (i + 1) % count) for i in range(count)]
    behind = [(i, (i - 1) % count) for i in range(count)]
    from_left = lax.ppermute(source, axis, ahead)
    from_right = lax.ppermute(source, axis, behind)
    cut = source.shape[0] // 2
    far = jnp.concatenate(
        [lax.ppermute(from_left[:cut], axis, ahead), lax.ppermute(from_right[cut:], axis, behind)],
        axis=0,
    )
    placed = jnp.zeros((count,) + source.shape, source.dtype)
    for step, part in ((0, source), (1, from_right), (2, far), (3, from_left)):
        where = ((me + step) % count,) + (0,) * source.ndim
        placed = lax.dynamic_update_slice(placed, part[None], where)
    if inner is None:
        return placed
    return placed.reshape((-1,) + source.shape[1:])


def attend(queries, fresh_key, value_new, keys, values, positions):
    beams = queries.shape[0]
    grouped_heads = queries.reshape(beams, KVH, QH // KVH, HD)
    scale_factor = HD ** (-0.5)
    scores = (
        jnp.einsum("bkgd,btkd->bkgt", grouped_heads, keys, preferred_element_type=jnp.float32)
        * scale_factor
    )
    local_beam_score = (
        jnp.einsum("rhap,rhp->rha", grouped_heads, fresh_key, preferred_element_type=jnp.float32)
        * scale_factor
    )
    valid = (jnp.arange(keys.shape[1], dtype=jnp.int32)[None, :] < positions[:, None])[
        :, None, None, :
    ]
    scores = jnp.where(valid, scores, -1e30)
    highest = jnp.maximum(jnp.max(scores, axis=-1), local_beam_score)
    weights = jnp.where(valid, jnp.exp(scores - highest[..., None]), 0.0)
    own_weight = jnp.exp(local_beam_score - highest)
    totals = jnp.sum(weights, axis=-1) + own_weight
    probs = (weights / totals[..., None]).astype(jnp.bfloat16)
    own_prob = (own_weight / totals).astype(jnp.bfloat16)
    output = jnp.einsum("bkgt,btkd->bkgd", probs, values, preferred_element_type=jnp.float32)
    output = (
        output
        + own_prob.astype(jnp.float32)[..., None] * value_new.astype(jnp.float32)[:, :, None, :]
    )
    return output.reshape(beams, QH * HD).astype(jnp.bfloat16)


def shards(hidden, norm_gain, w_qkv, w_out, kv_cache, lengths, kept_parent_device, keep_block):
    columns = lax.axis_size(BEAM)
    my_column = lax.axis_index(BEAM)
    grouped_row_block = hidden.shape[0]
    own_beams = grouped_row_block // columns
    cores = lax.axis_size("c")
    core = lax.axis_index("c")
    assert cores == 2
    halves = w_out.reshape(w_out.shape[0], cores, w_out.shape[1] // cores)
    mine = jnp.take(halves, core, axis=1)
    other = lax.ppermute(jnp.take(halves, 1 - core, axis=1), "c", [(0, 1), (1, 0)])
    w_local = jnp.where(core == 0, jnp.concatenate([mine, other], 0), jnp.concatenate([other, mine], 0))
    floats = hidden.astype(jnp.float32)
    scale_rms = lax.rsqrt(jnp.mean(floats * floats, axis=-1, keepdims=True) + 1e-05)
    normed = (floats * scale_rms * norm_gain.astype(jnp.float32)).astype(jnp.bfloat16)
    stack = gather_rows(w_qkv, "yh", lax.axis_size("yh"))
    w_local, stack = lax.optimization_barrier((w_local, stack))
    w_blocks = place_ring(w_local, "x", place_ring(w_local, "yh", None))
    xs = lax.axis_size("x")
    assert xs == 4
    me = lax.axis_index("x")
    ahead = [(i, (i + 1) % xs) for i in range(xs)]
    behind = [(i, (i - 1) % xs) for i in range(xs)]
    from_left = lax.ppermute(stack, "x", ahead)
    from_right = lax.ppermute(stack, "x", behind)
    cut = stack.shape[0] // 2
    far = jnp.concatenate(
        [lax.ppermute(from_left[:cut], "x", ahead), lax.ppermute(from_right[cut:], "x", behind)],
        axis=0,
    )
    rows = stack.shape[0]
    projected = None
    for step, piece in ((0, stack), (1, from_right), (3, from_left), (2, far)):
        start = ((me + step) % xs) * rows
        block = lax.dynamic_slice_in_dim(normed, start, rows, axis=1)
        term = jnp.einsum(
            "jbd,dc->bjc",
            block.reshape(columns, own_beams, rows),
            piece,
            preferred_element_type=jnp.float32,
        )
        projected = term if projected is None else projected + term
    own_qkv = regroup(projected.astype(jnp.bfloat16)).reshape(own_beams, QKV)
    blk_dev = kv_cache.shape[0]
    most_slots = max(2, 2 * blk_dev // columns)
    sources = kept_parent_device.reshape(columns, blk_dev)
    picked = keep_block.reshape(columns, blk_dev)
    is_mine = (sources == my_column).astype(jnp.int32)
    ranks = jnp.cumsum(is_mine, axis=1) - 1
    slot_ids = jnp.arange(most_slots, dtype=jnp.int32)
    chosen = is_mine[:, :, None] * (ranks[:, :, None] == slot_ids[None, None, :]).astype(jnp.int32)
    send_table = jnp.sum(chosen * picked[:, :, None], axis=1)
    outgoing = kv_cache[send_table.reshape(-1)].reshape((columns, most_slots) + kv_cache.shape[1:])
    incoming_blocks = lax.all_to_all(outgoing, BEAM, split_axis=0, concat_axis=0, tiled=True)
    own_sources = lax.dynamic_index_in_dim(sources, my_column, 0, keepdims=False)
    one_hot = (own_sources[:, None] == jnp.arange(columns, dtype=jnp.int32)[None, :]).astype(
        jnp.int32
    )
    earlier = jnp.cumsum(one_hot, axis=0) - one_hot
    arrival = jnp.sum(earlier * one_hot, axis=1)
    flat_blocks = incoming_blocks.reshape((columns * most_slots,) + kv_cache.shape[1:])
    moved = flat_blocks[own_sources * most_slots + arrival]
    moved = moved.reshape(own_beams, CACHE // PAGE, 2, PAGE, KVH, HD)
    keys = moved[:, :, 0].reshape(own_beams, CACHE, KVH, HD)
    values = moved[:, :, 1].reshape(own_beams, CACHE, KVH, HD)
    positions = lax.dynamic_slice_in_dim(lengths, my_column * own_beams, own_beams)
    query_cols = own_qkv[:, : QH * HD].reshape(own_beams, QH, HD).astype(jnp.float32)
    key_cols = own_qkv[:, QH * HD : (QH + KVH) * HD].reshape(own_beams, KVH, HD).astype(jnp.float32)
    value_new = own_qkv[:, (QH + KVH) * HD :].reshape(own_beams, KVH, HD)
    queries = rotary_embed(query_cols, positions).astype(jnp.bfloat16)
    fresh_key = rotary_embed(key_cols, positions).astype(jnp.bfloat16)
    attn = attend(queries, fresh_key, value_new, keys, values, positions)
    pairs = columns // cores
    pair_feats = attn.reshape(own_beams, pairs, 1, cores * attn.shape[1] // columns)
    doubled = jnp.broadcast_to(pair_feats, (own_beams, pairs, cores, pair_feats.shape[3]))
    head_rows = lax.all_to_all(
        doubled.reshape(own_beams, columns, pair_feats.shape[3]), BEAM, 1, 1, tiled=True
    )
    block = attn.shape[1] // columns
    partial = None
    for half in range(cores):
        term = jnp.einsum(
            "bjh,phc->jbpc",
            head_rows[:, :, half * block : (half + 1) * block],
            w_blocks[:, half * block : (half + 1) * block],
            preferred_element_type=jnp.float32,
        ).astype(jnp.bfloat16).astype(jnp.float32)
        partial = term if partial is None else partial + term
    partial = partial.astype(jnp.bfloat16).reshape(grouped_row_block, pairs, block)
    spread = lax.all_to_all(partial.transpose(1, 0, 2), PAIR, 0, 0, tiled=True)
    return jnp.sum(spread.astype(jnp.float32), axis=0).astype(jnp.bfloat16)


def solution(mesh):
    sizes = dict(mesh.shape)
    parts = mesh.devices.reshape(4, sizes["owner"] // 4, 2, sizes["beam"] // 4, 2)
    view = Mesh(parts, OWNER + BEAM)
    return jax.shard_map(
        shards,
        mesh=view,
        in_specs=(
            P(OWNER, None),
            P(),
            P(OWNER, BEAM),
            P(BEAM, OWNER),
            P(OWNER + BEAM, None, None, None),
            P(OWNER),
            P(OWNER, None),
            P(OWNER),
        ),
        out_specs=P(OWNER, BEAM),
        check_vma=False,
    )
```

```python
import jax
import jax.numpy as jnp
from jax import lax
from jax.sharding import Mesh
from jax.sharding import PartitionSpec as P

QH = 64
KVH = 8
HD = 128
CACHE = 32
PAGE = 8
QKV = 10240

OWNER = ("x", "yh")
BEAM = ("yl", "z", "c")
PAIR = ("yl", "z")


def rotary_embed(values, positions):
    half = values.shape[-1] // 2
    freqs = 500000.0 ** (-(jnp.arange(half, dtype=jnp.float32) * 2.0) / values.shape[-1])
    angles = positions.astype(jnp.float32)[:, None] * freqs[None, :]
    cosine = jnp.cos(angles)[:, None, :]
    sine = jnp.sin(angles)[:, None, :]
    first = values[..., :half]
    second = values[..., half:]
    return jnp.concatenate(
        [first * cosine - second * sine, second * cosine + first * sine], axis=-1
    )


def regroup(blocks):
    return lax.all_to_all(blocks, BEAM, split_axis=1, concat_axis=1, tiled=True)


def gather_rows(tile, axis, count):
    copies = jnp.broadcast_to(tile[None], (count,) + tile.shape)
    return lax.all_to_all(copies, axis, 0, 0, tiled=True).reshape((-1,) + tile.shape[1:])


def attend(queries, fresh_key, value_new, keys, values, positions):
    beams = queries.shape[0]
    grouped_heads = queries.reshape(beams, KVH, QH // KVH, HD)
    scale_factor = HD ** (-0.5)
    scores = (
        jnp.einsum("bkgd,btkd->bkgt", grouped_heads, keys, preferred_element_type=jnp.float32)
        * scale_factor
    )
    local_beam_score = (
        jnp.einsum("rhap,rhp->rha", grouped_heads, fresh_key, preferred_element_type=jnp.float32)
        * scale_factor
    )
    valid = (jnp.arange(keys.shape[1], dtype=jnp.int32)[None, :] < positions[:, None])[
        :, None, None, :
    ]
    scores = jnp.where(valid, scores, -1e30)
    highest = jnp.maximum(jnp.max(scores, axis=-1), local_beam_score)
    weights = jnp.where(valid, jnp.exp(scores - highest[..., None]), 0.0)
    own_weight = jnp.exp(local_beam_score - highest)
    totals = jnp.sum(weights, axis=-1) + own_weight
    probs = (weights / totals[..., None]).astype(jnp.bfloat16)
    own_prob = (own_weight / totals).astype(jnp.bfloat16)
    output = jnp.einsum("bkgt,btkd->bkgd", probs, values, preferred_element_type=jnp.float32)
    output = (
        output
        + own_prob.astype(jnp.float32)[..., None] * value_new.astype(jnp.float32)[:, :, None, :]
    )
    return output.reshape(beams, QH * HD).astype(jnp.bfloat16)


def shards(hidden, norm_gain, w_qkv, w_out, kv_cache, lengths, kept_parent_device, keep_block):
    columns = lax.axis_size(BEAM)
    my_column = lax.axis_index(BEAM)
    grouped_row_block = hidden.shape[0]
    own_beams = grouped_row_block // columns
    cores = lax.axis_size("c")
    core = lax.axis_index("c")
    assert cores == 2
    halves = w_out.reshape(w_out.shape[0], cores, w_out.shape[1] // cores)
    mine = jnp.take(halves, core, axis=1)
    other = lax.ppermute(jnp.take(halves, 1 - core, axis=1), "c", [(0, 1), (1, 0)])
    w_local = jnp.where(core == 0, jnp.concatenate([mine, other], 0), jnp.concatenate([other, mine], 0))
    floats = hidden.astype(jnp.float32)
    scale_rms = lax.rsqrt(jnp.mean(floats * floats, axis=-1, keepdims=True) + 1e-05)
    normed = (floats * scale_rms * norm_gain.astype(jnp.float32)).astype(jnp.bfloat16)
    stack = gather_rows(w_qkv, "yh", lax.axis_size("yh"))
    xs = lax.axis_size("x")
    assert xs == 4
    me = lax.axis_index("x")
    ahead = [(i, (i + 1) % xs) for i in range(xs)]
    behind = [(i, (i - 1) % xs) for i in range(xs)]
    from_left = lax.ppermute(stack, "x", ahead)
    from_right = lax.ppermute(stack, "x", behind)
    w_local, from_left, from_right = lax.optimization_barrier((w_local, from_left, from_right))
    w_pair = lax.all_gather(w_local[:, None], OWNER, axis=1, tiled=True)
    cut = stack.shape[0] // 2
    far = jnp.concatenate(
        [lax.ppermute(from_left[:cut], "x", ahead), lax.ppermute(from_right[cut:], "x", behind)],
        axis=0,
    )
    rows = stack.shape[0]
    projected = None
    for step, piece in ((0, stack), (1, from_right), (3, from_left), (2, far)):
        start = ((me + step) % xs) * rows
        block = lax.dynamic_slice_in_dim(normed, start, rows, axis=1)
        term = jnp.einsum(
            "jbd,dc->bjc",
            block.reshape(columns, own_beams, rows),
            piece,
            preferred_element_type=jnp.float32,
        )
        projected = term if projected is None else projected + term
    own_qkv = regroup(projected.astype(jnp.bfloat16)).reshape(own_beams, QKV)
    blk_dev = kv_cache.shape[0]
    most_slots = max(2, 2 * blk_dev // columns)
    sources = kept_parent_device.reshape(columns, blk_dev)
    picked = keep_block.reshape(columns, blk_dev)
    is_mine = (sources == my_column).astype(jnp.int32)
    ranks = jnp.cumsum(is_mine, axis=1) - 1
    slot_ids = jnp.arange(most_slots, dtype=jnp.int32)
    chosen = is_mine[:, :, None] * (ranks[:, :, None] == slot_ids[None, None, :]).astype(jnp.int32)
    send_table = jnp.sum(chosen * picked[:, :, None], axis=1)
    outgoing = kv_cache[send_table.reshape(-1)].reshape((columns, most_slots) + kv_cache.shape[1:])
    incoming_blocks = lax.all_to_all(outgoing, BEAM, split_axis=0, concat_axis=0, tiled=True)
    own_sources = lax.dynamic_index_in_dim(sources, my_column, 0, keepdims=False)
    one_hot = (own_sources[:, None] == jnp.arange(columns, dtype=jnp.int32)[None, :]).astype(
        jnp.int32
    )
    earlier = jnp.cumsum(one_hot, axis=0) - one_hot
    arrival = jnp.sum(earlier * one_hot, axis=1)
    flat_blocks = incoming_blocks.reshape((columns * most_slots,) + kv_cache.shape[1:])
    moved = flat_blocks[own_sources * most_slots + arrival]
    moved = moved.reshape(own_beams, CACHE // PAGE, 2, PAGE, KVH, HD)
    keys = moved[:, :, 0].reshape(own_beams, CACHE, KVH, HD)
    values = moved[:, :, 1].reshape(own_beams, CACHE, KVH, HD)
    positions = lax.dynamic_slice_in_dim(lengths, my_column * own_beams, own_beams)
    query_cols = own_qkv[:, : QH * HD].reshape(own_beams, QH, HD).astype(jnp.float32)
    key_cols = own_qkv[:, QH * HD : (QH + KVH) * HD].reshape(own_beams, KVH, HD).astype(jnp.float32)
    value_new = own_qkv[:, (QH + KVH) * HD :].reshape(own_beams, KVH, HD)
    queries = rotary_embed(query_cols, positions).astype(jnp.bfloat16)
    fresh_key = rotary_embed(key_cols, positions).astype(jnp.bfloat16)
    attn = attend(queries, fresh_key, value_new, keys, values, positions)
    pairs = columns // cores
    block = attn.shape[1] // columns
    own_rows = regroup(attn.reshape(own_beams, columns, block))
    sib_rows = lax.ppermute(own_rows, "c", [(0, 1), (1, 0)])
    first = jnp.where(core == 0, own_rows, sib_rows)
    second = jnp.where(core == 0, sib_rows, own_rows)
    partial = None
    for half in range(cores):
        term = jnp.einsum(
            "bjh,hpc->jbpc",
            (first, second)[half],
            w_pair[half * block : (half + 1) * block],
            preferred_element_type=jnp.float32,
        ).astype(jnp.bfloat16).astype(jnp.float32)
        partial = term if partial is None else partial + term
    partial = partial.astype(jnp.bfloat16).reshape(grouped_row_block, pairs, block)
    spread = lax.all_to_all(partial.transpose(1, 0, 2), PAIR, 0, 0, tiled=True)
    return jnp.sum(spread.astype(jnp.float32), axis=0).astype(jnp.bfloat16)


def solution(mesh):
    sizes = dict(mesh.shape)
    parts = mesh.devices.reshape(4, sizes["owner"] // 4, 2, sizes["beam"] // 4, 2)
    view = Mesh(parts, OWNER + BEAM)
    return jax.shard_map(
        shards,
        mesh=view,
        in_specs=(
            P(OWNER, None),
            P(),
            P(OWNER, BEAM),
            P(BEAM, OWNER),
            P(OWNER + BEAM, None, None, None),
            P(OWNER),
            P(OWNER, None),
            P(OWNER),
        ),
        out_specs=P(OWNER, BEAM),
        check_vma=False,
    )
```

```python
import jax
import jax.numpy as jnp
from jax import lax
from jax.sharding import Mesh
from jax.sharding import PartitionSpec as P

QH = 64
KVH = 8
HD = 128
CACHE = 32
PAGE = 8
QKV = 10240

OWNER = ("x", "yh")
BEAM = ("yl", "z", "c")
PAIR = ("yl", "z")


def rotary_embed(values, positions):
    half = values.shape[-1] // 2
    freqs = 500000.0 ** (-(jnp.arange(half, dtype=jnp.float32) * 2.0) / values.shape[-1])
    angles = positions.astype(jnp.float32)[:, None] * freqs[None, :]
    cosine = jnp.cos(angles)[:, None, :]
    sine = jnp.sin(angles)[:, None, :]
    first = values[..., :half]
    second = values[..., half:]
    return jnp.concatenate(
        [first * cosine - second * sine, second * cosine + first * sine], axis=-1
    )


def regroup(blocks):
    return lax.all_to_all(blocks, BEAM, split_axis=1, concat_axis=1, tiled=True)


def gather_rows(tile, axis, count):
    copies = jnp.broadcast_to(tile[None], (count,) + tile.shape)
    return lax.all_to_all(copies, axis, 0, 0, tiled=True).reshape((-1,) + tile.shape[1:])


def attend(queries, fresh_key, value_new, keys, values, positions):
    beams = queries.shape[0]
    grouped_heads = queries.reshape(beams, KVH, QH // KVH, HD)
    scale_factor = HD ** (-0.5)
    scores = (
        jnp.einsum("bkgd,btkd->bkgt", grouped_heads, keys, preferred_element_type=jnp.float32)
        * scale_factor
    )
    local_beam_score = (
        jnp.einsum("rhap,rhp->rha", grouped_heads, fresh_key, preferred_element_type=jnp.float32)
        * scale_factor
    )
    valid = (jnp.arange(keys.shape[1], dtype=jnp.int32)[None, :] < positions[:, None])[
        :, None, None, :
    ]
    scores = jnp.where(valid, scores, -1e30)
    highest = jnp.maximum(jnp.max(scores, axis=-1), local_beam_score)
    weights = jnp.where(valid, jnp.exp(scores - highest[..., None]), 0.0)
    own_weight = jnp.exp(local_beam_score - highest)
    totals = jnp.sum(weights, axis=-1) + own_weight
    probs = (weights / totals[..., None]).astype(jnp.bfloat16)
    own_prob = (own_weight / totals).astype(jnp.bfloat16)
    output = jnp.einsum("bkgt,btkd->bkgd", probs, values, preferred_element_type=jnp.float32)
    output = (
        output
        + own_prob.astype(jnp.float32)[..., None] * value_new.astype(jnp.float32)[:, :, None, :]
    )
    return output.reshape(beams, QH * HD).astype(jnp.bfloat16)


def shards(hidden, norm_gain, w_qkv, w_out, kv_cache, lengths, kept_parent_device, keep_block):
    columns = lax.axis_size(BEAM)
    my_column = lax.axis_index(BEAM)
    grouped_row_block = hidden.shape[0]
    own_beams = grouped_row_block // columns
    cores = lax.axis_size("c")
    core = lax.axis_index("c")
    assert cores == 2
    halves = w_out.reshape(w_out.shape[0], cores, w_out.shape[1] // cores)
    mine = jnp.take(halves, core, axis=1)
    other = lax.ppermute(jnp.take(halves, 1 - core, axis=1), "c", [(0, 1), (1, 0)])
    w_local = jnp.where(core == 0, jnp.concatenate([mine, other], 0), jnp.concatenate([other, mine], 0))
    floats = hidden.astype(jnp.float32)
    scale_rms = lax.rsqrt(jnp.mean(floats * floats, axis=-1, keepdims=True) + 1e-05)
    normed = (floats * scale_rms * norm_gain.astype(jnp.float32)).astype(jnp.bfloat16)
    stack = gather_rows(w_qkv, "yh", lax.axis_size("yh"))
    xs = lax.axis_size("x")
    assert xs == 4
    me = lax.axis_index("x")
    ahead = [(i, (i + 1) % xs) for i in range(xs)]
    behind = [(i, (i - 1) % xs) for i in range(xs)]
    from_left = lax.ppermute(stack, "x", ahead)
    from_right = lax.ppermute(stack, "x", behind)
    w_local, from_left, from_right = lax.optimization_barrier((w_local, from_left, from_right))
    w_pair = lax.all_gather(w_local[:, None], OWNER, axis=1, tiled=True)
    cut = stack.shape[0] // 2
    far = jnp.concatenate(
        [lax.ppermute(from_left[:cut], "x", ahead), lax.ppermute(from_right[cut:], "x", behind)],
        axis=0,
    )
    rows = stack.shape[0]
    projected = None
    for step, piece in ((0, stack), (1, from_right), (3, from_left), (2, far)):
        start = ((me + step) % xs) * rows
        block = lax.dynamic_slice_in_dim(normed, start, rows, axis=1)
        term = jnp.einsum(
            "jbd,dc->bjc",
            block.reshape(columns, own_beams, rows),
            piece,
            preferred_element_type=jnp.float32,
        )
        projected = term if projected is None else projected + term
    own_qkv = regroup(projected.astype(jnp.bfloat16)).reshape(own_beams, QKV)
    blk_dev = kv_cache.shape[0]
    most_slots = max(2, 2 * blk_dev // columns)
    sources = kept_parent_device.reshape(columns, blk_dev)
    picked = keep_block.reshape(columns, blk_dev)
    is_mine = (sources == my_column).astype(jnp.int32)
    ranks = jnp.cumsum(is_mine, axis=1) - 1
    slot_ids = jnp.arange(most_slots, dtype=jnp.int32)
    chosen = is_mine[:, :, None] * (ranks[:, :, None] == slot_ids[None, None, :]).astype(jnp.int32)
    send_table = jnp.sum(chosen * picked[:, :, None], axis=1)
    outgoing = kv_cache[send_table.reshape(-1)].reshape((columns, most_slots) + kv_cache.shape[1:])
    incoming_blocks = lax.all_to_all(outgoing, BEAM, split_axis=0, concat_axis=0, tiled=True)
    own_sources = lax.dynamic_index_in_dim(sources, my_column, 0, keepdims=False)
    one_hot = (own_sources[:, None] == jnp.arange(columns, dtype=jnp.int32)[None, :]).astype(
        jnp.int32
    )
    earlier = jnp.cumsum(one_hot, axis=0) - one_hot
    arrival = jnp.sum(earlier * one_hot, axis=1)
    flat_blocks = incoming_blocks.reshape((columns * most_slots,) + kv_cache.shape[1:])
    moved = flat_blocks[own_sources * most_slots + arrival]
    moved = moved.reshape(own_beams, CACHE // PAGE, 2, PAGE, KVH, HD)
    keys = moved[:, :, 0].reshape(own_beams, CACHE, KVH, HD)
    values = moved[:, :, 1].reshape(own_beams, CACHE, KVH, HD)
    positions = lax.dynamic_slice_in_dim(lengths, my_column * own_beams, own_beams)
    query_cols = own_qkv[:, : QH * HD].reshape(own_beams, QH, HD).astype(jnp.float32)
    key_cols = own_qkv[:, QH * HD : (QH + KVH) * HD].reshape(own_beams, KVH, HD).astype(jnp.float32)
    value_new = own_qkv[:, (QH + KVH) * HD :].reshape(own_beams, KVH, HD)
    queries = rotary_embed(query_cols, positions).astype(jnp.bfloat16)
    fresh_key = rotary_embed(key_cols, positions).astype(jnp.bfloat16)
    attn = attend(queries, fresh_key, value_new, keys, values, positions)
    pairs = columns // cores
    pair_feats = attn.reshape(own_beams, pairs, 1, cores * attn.shape[1] // columns)
    doubled = jnp.broadcast_to(pair_feats, (own_beams, pairs, cores, pair_feats.shape[3]))
    head_rows = lax.all_to_all(
        doubled.reshape(own_beams, columns, pair_feats.shape[3]), BEAM, 1, 1, tiled=True
    )
    block = attn.shape[1] // columns
    partial = None
    for half in range(cores):
        term = jnp.einsum(
            "bjh,hpc->pjbc",
            head_rows[:, :, half * block : (half + 1) * block],
            w_pair[half * block : (half + 1) * block],
            preferred_element_type=jnp.float32,
        ).astype(jnp.bfloat16).astype(jnp.float32)
        partial = term if partial is None else partial + term
    partial = partial.astype(jnp.bfloat16).reshape(pairs, grouped_row_block, block)
    spread = lax.all_to_all(partial, PAIR, 0, 0, tiled=True)
    return jnp.sum(spread.astype(jnp.float32), axis=0).astype(jnp.bfloat16)


def solution(mesh):
    sizes = dict(mesh.shape)
    parts = mesh.devices.reshape(4, sizes["owner"] // 4, 2, sizes["beam"] // 4, 2)
    view = Mesh(parts, OWNER + BEAM)
    return jax.shard_map(
        shards,
        mesh=view,
        in_specs=(
            P(OWNER, None),
            P(),
            P(OWNER, BEAM),
            P(BEAM, OWNER),
            P(OWNER + BEAM, None, None, None),
            P(OWNER),
            P(OWNER, None),
            P(OWNER),
        ),
        out_specs=P(OWNER, BEAM),
        check_vma=False,
    )
```

```python
import jax
import jax.numpy as jnp
from jax import lax
from jax.sharding import Mesh
from jax.sharding import PartitionSpec as P

QH = 64
KVH = 8
HD = 128
CACHE = 32
PAGE = 8
QKV = 10240

OWNER = ("x", "yh")
BEAM = ("yl", "z", "c")
PAIR = ("yl", "z")


def rotary_embed(values, positions):
    half = values.shape[-1] // 2
    freqs = 500000.0 ** (-(jnp.arange(half, dtype=jnp.float32) * 2.0) / values.shape[-1])
    angles = positions.astype(jnp.float32)[:, None] * freqs[None, :]
    cosine = jnp.cos(angles)[:, None, :]
    sine = jnp.sin(angles)[:, None, :]
    first = values[..., :half]
    second = values[..., half:]
    return jnp.concatenate(
        [first * cosine - second * sine, second * cosine + first * sine], axis=-1
    )


def regroup(blocks):
    return lax.all_to_all(blocks, BEAM, split_axis=1, concat_axis=1, tiled=True)


def gather_rows(tile, axis, count):
    copies = jnp.broadcast_to(tile[None], (count,) + tile.shape)
    return lax.all_to_all(copies, axis, 0, 0, tiled=True).reshape((-1,) + tile.shape[1:])


def attend(queries, fresh_key, value_new, keys, values, positions):
    beams = queries.shape[0]
    grouped_heads = queries.reshape(beams, KVH, QH // KVH, HD)
    scale_factor = HD ** (-0.5)
    scores = (
        jnp.einsum("bkgd,btkd->bkgt", grouped_heads, keys, preferred_element_type=jnp.float32)
        * scale_factor
    )
    local_beam_score = (
        jnp.einsum("rhap,rhp->rha", grouped_heads, fresh_key, preferred_element_type=jnp.float32)
        * scale_factor
    )
    valid = (jnp.arange(keys.shape[1], dtype=jnp.int32)[None, :] < positions[:, None])[
        :, None, None, :
    ]
    scores = jnp.where(valid, scores, -1e30)
    highest = jnp.maximum(jnp.max(scores, axis=-1), local_beam_score)
    weights = jnp.where(valid, jnp.exp(scores - highest[..., None]), 0.0)
    own_weight = jnp.exp(local_beam_score - highest)
    totals = jnp.sum(weights, axis=-1) + own_weight
    probs = (weights / totals[..., None]).astype(jnp.bfloat16)
    own_prob = (own_weight / totals).astype(jnp.bfloat16)
    output = jnp.einsum("bkgt,btkd->bkgd", probs, values, preferred_element_type=jnp.float32)
    output = (
        output
        + own_prob.astype(jnp.float32)[..., None] * value_new.astype(jnp.float32)[:, :, None, :]
    )
    return output.reshape(beams, QH * HD).astype(jnp.bfloat16)


def shards(hidden, norm_gain, w_qkv, w_out, kv_cache, lengths, kept_parent_device, keep_block):
    columns = lax.axis_size(BEAM)
    my_column = lax.axis_index(BEAM)
    grouped_row_block = hidden.shape[0]
    own_beams = grouped_row_block // columns
    cores = lax.axis_size("c")
    core = lax.axis_index("c")
    assert cores == 2
    halves = w_out.reshape(w_out.shape[0], cores, w_out.shape[1] // cores)
    mine = jnp.take(halves, core, axis=1)
    other = lax.ppermute(jnp.take(halves, 1 - core, axis=1), "c", [(0, 1), (1, 0)])
    w_local = jnp.where(core == 0, jnp.concatenate([mine, other], 0), jnp.concatenate([other, mine], 0))
    floats = hidden.astype(jnp.float32)
    scale_rms = lax.rsqrt(jnp.mean(floats * floats, axis=-1, keepdims=True) + 1e-05)
    normed = (floats * scale_rms * norm_gain.astype(jnp.float32)).astype(jnp.bfloat16)
    stack = gather_rows(w_qkv, "yh", lax.axis_size("yh"))
    xs = lax.axis_size("x")
    assert xs == 4
    me = lax.axis_index("x")
    ahead = [(i, (i + 1) % xs) for i in range(xs)]
    behind = [(i, (i - 1) % xs) for i in range(xs)]
    from_left = lax.ppermute(stack, "x", ahead)
    from_right = lax.ppermute(stack, "x", behind)
    w_local, from_left, from_right = lax.optimization_barrier((w_local, from_left, from_right))
    w_pair = lax.all_gather(w_local[:, None], OWNER, axis=1, tiled=True)
    cut = stack.shape[0] // 2
    far = jnp.concatenate(
        [lax.ppermute(from_left[:cut], "x", ahead), lax.ppermute(from_right[cut:], "x", behind)],
        axis=0,
    )
    rows = stack.shape[0]
    projected = None
    for step, piece in ((0, stack), (1, from_right), (3, from_left), (2, far)):
        start = ((me + step) % xs) * rows
        block = lax.dynamic_slice_in_dim(normed, start, rows, axis=1)
        term = jnp.einsum(
            "jbd,dc->bjc",
            block.reshape(columns, own_beams, rows),
            piece,
            preferred_element_type=jnp.float32,
        )
        projected = term if projected is None else projected + term
    own_qkv = regroup(projected.astype(jnp.bfloat16)).reshape(own_beams, QKV)
    blk_dev = kv_cache.shape[0]
    most_slots = max(2, 2 * blk_dev // columns)
    sources = kept_parent_device.reshape(columns, blk_dev)
    picked = keep_block.reshape(columns, blk_dev)
    is_mine = (sources == my_column).astype(jnp.int32)
    ranks = jnp.cumsum(is_mine, axis=1) - 1
    slot_ids = jnp.arange(most_slots, dtype=jnp.int32)
    chosen = is_mine[:, :, None] * (ranks[:, :, None] == slot_ids[None, None, :]).astype(jnp.int32)
    send_table = jnp.sum(chosen * picked[:, :, None], axis=1)
    outgoing = kv_cache[send_table.reshape(-1)].reshape((columns, most_slots) + kv_cache.shape[1:])
    incoming_blocks = lax.all_to_all(outgoing, BEAM, split_axis=0, concat_axis=0, tiled=True)
    own_sources = lax.dynamic_index_in_dim(sources, my_column, 0, keepdims=False)
    one_hot = (own_sources[:, None] == jnp.arange(columns, dtype=jnp.int32)[None, :]).astype(
        jnp.int32
    )
    earlier = jnp.cumsum(one_hot, axis=0) - one_hot
    arrival = jnp.sum(earlier * one_hot, axis=1)
    flat_blocks = incoming_blocks.reshape((columns * most_slots,) + kv_cache.shape[1:])
    moved = flat_blocks[own_sources * most_slots + arrival]
    moved = moved.reshape(own_beams, CACHE // PAGE, 2, PAGE, KVH, HD)
    keys = moved[:, :, 0].reshape(own_beams, CACHE, KVH, HD)
    values = moved[:, :, 1].reshape(own_beams, CACHE, KVH, HD)
    positions = lax.dynamic_slice_in_dim(lengths, my_column * own_beams, own_beams)
    query_cols = own_qkv[:, : QH * HD].reshape(own_beams, QH, HD).astype(jnp.float32)
    key_cols = own_qkv[:, QH * HD : (QH + KVH) * HD].reshape(own_beams, KVH, HD).astype(jnp.float32)
    value_new = own_qkv[:, (QH + KVH) * HD :].reshape(own_beams, KVH, HD)
    queries = rotary_embed(query_cols, positions).astype(jnp.bfloat16)
    fresh_key = rotary_embed(key_cols, positions).astype(jnp.bfloat16)
    attn = attend(queries, fresh_key, value_new, keys, values, positions)
    pairs = columns // cores
    pair_feats = attn.reshape(own_beams, pairs, 1, cores * attn.shape[1] // columns)
    doubled = jnp.broadcast_to(pair_feats, (own_beams, pairs, cores, pair_feats.shape[3]))
    head_rows = lax.all_to_all(
        doubled.reshape(own_beams, columns, pair_feats.shape[3]), BEAM, 1, 1, tiled=True
    )
    block = attn.shape[1] // columns
    halves_out = jnp.einsum(
        "bjkh,khpc->kpjbc",
        head_rows.reshape(own_beams, columns, cores, block),
        w_pair.reshape(cores, block, pairs, block),
        preferred_element_type=jnp.float32,
    )
    partial = jnp.sum(halves_out.astype(jnp.bfloat16).astype(jnp.float32), axis=0)
    partial = partial.astype(jnp.bfloat16).reshape(pairs, grouped_row_block, block)
    spread = lax.all_to_all(partial, PAIR, 0, 0, tiled=True)
    return jnp.sum(spread.astype(jnp.float32), axis=0).astype(jnp.bfloat16)


def solution(mesh):
    sizes = dict(mesh.shape)
    parts = mesh.devices.reshape(4, sizes["owner"] // 4, 2, sizes["beam"] // 4, 2)
    view = Mesh(parts, OWNER + BEAM)
    return jax.shard_map(
        shards,
        mesh=view,
        in_specs=(
            P(OWNER, None),
            P(),
            P(OWNER, BEAM),
            P(BEAM, OWNER),
            P(OWNER + BEAM, None, None, None),
            P(OWNER),
            P(OWNER, None),
            P(OWNER),
        ),
        out_specs=P(OWNER, BEAM),
        check_vma=False,
    )
```

```python
import jax
import jax.numpy as jnp
from jax import lax
from jax.sharding import Mesh
from jax.sharding import PartitionSpec as P

QH = 64
KVH = 8
HD = 128
CACHE = 32
PAGE = 8
QKV = 10240

OWNER = ("x", "yh")
BEAM = ("yl", "z", "c")
PAIR = ("yl", "z")


def rotary_embed(values, positions):
    half = values.shape[-1] // 2
    freqs = 500000.0 ** (-(jnp.arange(half, dtype=jnp.float32) * 2.0) / values.shape[-1])
    angles = positions.astype(jnp.float32)[:, None] * freqs[None, :]
    cosine = jnp.cos(angles)[:, None, :]
    sine = jnp.sin(angles)[:, None, :]
    first = values[..., :half]
    second = values[..., half:]
    return jnp.concatenate(
        [first * cosine - second * sine, second * cosine + first * sine], axis=-1
    )


def regroup(blocks):
    return lax.all_to_all(blocks, BEAM, split_axis=1, concat_axis=1, tiled=True)


def gather_rows(tile, axis, count):
    copies = jnp.broadcast_to(tile[None], (count,) + tile.shape)
    return lax.all_to_all(copies, axis, 0, 0, tiled=True).reshape((-1,) + tile.shape[1:])


def attend(queries, fresh_key, value_new, keys, values, positions):
    beams = queries.shape[0]
    grouped_heads = queries.reshape(beams, KVH, QH // KVH, HD)
    scale_factor = HD ** (-0.5)
    scores = (
        jnp.einsum("bkgd,btkd->bkgt", grouped_heads, keys, preferred_element_type=jnp.float32)
        * scale_factor
    )
    local_beam_score = (
        jnp.einsum("rhap,rhp->rha", grouped_heads, fresh_key, preferred_element_type=jnp.float32)
        * scale_factor
    )
    valid = (jnp.arange(keys.shape[1], dtype=jnp.int32)[None, :] < positions[:, None])[
        :, None, None, :
    ]
    scores = jnp.where(valid, scores, -1e30)
    highest = jnp.maximum(jnp.max(scores, axis=-1), local_beam_score)
    weights = jnp.where(valid, jnp.exp(scores - highest[..., None]), 0.0)
    own_weight = jnp.exp(local_beam_score - highest)
    totals = jnp.sum(weights, axis=-1) + own_weight
    probs = (weights / totals[..., None]).astype(jnp.bfloat16)
    own_prob = (own_weight / totals).astype(jnp.bfloat16)
    output = jnp.einsum("bkgt,btkd->bkgd", probs, values, preferred_element_type=jnp.float32)
    output = (
        output
        + own_prob.astype(jnp.float32)[..., None] * value_new.astype(jnp.float32)[:, :, None, :]
    )
    return output.reshape(beams, QH * HD).astype(jnp.bfloat16)


def shards(hidden, norm_gain, w_qkv, w_out, kv_cache, lengths, kept_parent_device, keep_block):
    columns = lax.axis_size(BEAM)
    my_column = lax.axis_index(BEAM)
    grouped_row_block = hidden.shape[0]
    own_beams = grouped_row_block // columns
    cores = lax.axis_size("c")
    core = lax.axis_index("c")
    assert cores == 2
    halves = w_out.reshape(w_out.shape[0], cores, w_out.shape[1] // cores)
    mine = jnp.take(halves, core, axis=1)
    other = lax.ppermute(jnp.take(halves, 1 - core, axis=1), "c", [(0, 1), (1, 0)])
    w_local = jnp.where(core == 0, jnp.concatenate([mine, other], 0), jnp.concatenate([other, mine], 0))
    floats = hidden.astype(jnp.float32)
    scale_rms = lax.rsqrt(jnp.mean(floats * floats, axis=-1, keepdims=True) + 1e-05)
    normed = (floats * scale_rms * norm_gain.astype(jnp.float32)).astype(jnp.bfloat16)
    stack = gather_rows(w_qkv, "yh", lax.axis_size("yh"))
    xs = lax.axis_size("x")
    assert xs == 4
    me = lax.axis_index("x")
    ahead = [(i, (i + 1) % xs) for i in range(xs)]
    behind = [(i, (i - 1) % xs) for i in range(xs)]
    from_left = lax.ppermute(stack, "x", ahead)
    from_right = lax.ppermute(stack, "x", behind)
    w_local, from_left, from_right = lax.optimization_barrier((w_local, from_left, from_right))
    w_pair = lax.all_gather(w_local[:, None], OWNER, axis=1, tiled=True)
    cut = stack.shape[0] // 2
    far = jnp.concatenate(
        [lax.ppermute(from_left[:cut], "x", ahead), lax.ppermute(from_right[cut:], "x", behind)],
        axis=0,
    )
    rows = stack.shape[0]
    projected = None
    for step, piece in ((0, stack), (1, from_right), (3, from_left), (2, far)):
        start = ((me + step) % xs) * rows
        block = lax.dynamic_slice_in_dim(normed, start, rows, axis=1)
        term = jnp.einsum(
            "jbd,dc->bjc",
            block.reshape(columns, own_beams, rows),
            piece,
            preferred_element_type=jnp.float32,
        )
        projected = term if projected is None else projected + term
    own_qkv = regroup(projected.astype(jnp.bfloat16)).reshape(own_beams, QKV)
    blk_dev = kv_cache.shape[0]
    most_slots = max(2, 2 * blk_dev // columns)
    sources = kept_parent_device.reshape(columns, blk_dev)
    picked = keep_block.reshape(columns, blk_dev)
    is_mine = (sources == my_column).astype(jnp.int32)
    ranks = jnp.cumsum(is_mine, axis=1) - 1
    slot_ids = jnp.arange(most_slots, dtype=jnp.int32)
    chosen = is_mine[:, :, None] * (ranks[:, :, None] == slot_ids[None, None, :]).astype(jnp.int32)
    send_table = jnp.sum(chosen * picked[:, :, None], axis=1)
    outgoing = kv_cache[send_table.reshape(-1)].reshape((columns, most_slots) + kv_cache.shape[1:])
    incoming_blocks = lax.all_to_all(outgoing, BEAM, split_axis=0, concat_axis=0, tiled=True)
    own_sources = lax.dynamic_index_in_dim(sources, my_column, 0, keepdims=False)
    one_hot = (own_sources[:, None] == jnp.arange(columns, dtype=jnp.int32)[None, :]).astype(
        jnp.int32
    )
    earlier = jnp.cumsum(one_hot, axis=0) - one_hot
    arrival = jnp.sum(earlier * one_hot, axis=1)
    flat_blocks = incoming_blocks.reshape((columns * most_slots,) + kv_cache.shape[1:])
    moved = flat_blocks[own_sources * most_slots + arrival]
    moved = moved.reshape(own_beams, CACHE // PAGE, 2, PAGE, KVH, HD)
    keys = moved[:, :, 0].reshape(own_beams, CACHE, KVH, HD)
    values = moved[:, :, 1].reshape(own_beams, CACHE, KVH, HD)
    positions = lax.dynamic_slice_in_dim(lengths, my_column * own_beams, own_beams)
    query_cols = own_qkv[:, : QH * HD].reshape(own_beams, QH, HD).astype(jnp.float32)
    key_cols = own_qkv[:, QH * HD : (QH + KVH) * HD].reshape(own_beams, KVH, HD).astype(jnp.float32)
    value_new = own_qkv[:, (QH + KVH) * HD :].reshape(own_beams, KVH, HD)
    queries = rotary_embed(query_cols, positions).astype(jnp.bfloat16)
    fresh_key = rotary_embed(key_cols, positions).astype(jnp.bfloat16)
    attn = attend(queries, fresh_key, value_new, keys, values, positions)
    pairs = columns // cores
    pair_feats = attn.reshape(own_beams, pairs, 1, cores * attn.shape[1] // columns)
    doubled = jnp.broadcast_to(pair_feats, (own_beams, pairs, cores, pair_feats.shape[3]))
    head_rows = lax.all_to_all(
        doubled.reshape(own_beams, columns, pair_feats.shape[3]), BEAM, 1, 1, tiled=True
    )
    block = attn.shape[1] // columns
    partial = None
    for half in range(cores):
        term = jnp.einsum(
            "bjh,hpc->jbpc",
            head_rows[:, :, half * block : (half + 1) * block],
            w_pair[half * block : (half + 1) * block],
            preferred_element_type=jnp.float32,
        ).astype(jnp.bfloat16).astype(jnp.float32)
        partial = term if partial is None else partial + term
    partial = partial.astype(jnp.bfloat16).reshape(grouped_row_block, pairs, block)
    spread = lax.all_to_all(partial.transpose(1, 0, 2), PAIR, 0, 0, tiled=True)
    total = spread.astype(jnp.float32)
    while total.shape[0] > 1:
        count = total.shape[0] // 2
        total = total[:count] + total[count:]
    return total[0].astype(jnp.bfloat16)


def solution(mesh):
    sizes = dict(mesh.shape)
    parts = mesh.devices.reshape(4, sizes["owner"] // 4, 2, sizes["beam"] // 4, 2)
    view = Mesh(parts, OWNER + BEAM)
    return jax.shard_map(
        shards,
        mesh=view,
        in_specs=(
            P(OWNER, None),
            P(),
            P(OWNER, BEAM),
            P(BEAM, OWNER),
            P(OWNER + BEAM, None, None, None),
            P(OWNER),
            P(OWNER, None),
            P(OWNER),
        ),
        out_specs=P(OWNER, BEAM),
        check_vma=False,
    )
```
